128 devices in a mesh: resp: 8 (over x_lo, y), ctx: 16 (over z, x_hi, core).
Axes of the slice: x: 4 (x_hi: 2, x_lo: 2; x = x_hi * 2 + x_lo), y: 4, z: 4, core: 2. Of those that a mesh axis runs over, the one named last changes fastest.
Arguments:
- queries: bfloat16 [64, 512, 8192], P('resp', 'ctx'), may hold values from -32 to 32
- prompt_kv: bfloat16 [2, 1024, 1024], P(None, ('resp', 'ctx')), may hold values from -4 to 4
- response_kv: bfloat16 [2, 64, 512, 1024], P(None, 'resp', 'ctx'), may hold values from -4 to 4
- lengths: int32 [64], P('resp'), may hold values from 128 to 512, as said below
Outputs:
- attended: bfloat16 [64, 512, 8192], P('resp', 'ctx')
- row_lse: float32 [64, 512, 64], P('resp', 'ctx')
The draws below stay inside these ranges and needn't reach their ends.
Inputs may be any that keep to these rules, and one draw needn't show every extreme that they name: `lengths`: some response of every draw has length 512.
All inputs are finite; a program needn't handle non-finite values.
Results may differ from the reference program's by a relative error of at most 0.005.
Values may be sent and summed in bfloat16 or wider, within the bound.
No kernel may reach another device: no remote copies, remote signals or barrier semaphores. Data moves between devices by JAX's collectives and lax.ppermute only.
A program may use at most 256 MiB of HBM per device.

```python
import math
import jax
import jax.numpy as jnp
from jax import lax

HEADS = 64
KV_HEADS = 8
HEAD = 128
PROMPT = 1024
RESP = 64
LEN = 512


def draw_prompt_kv(key, part):
    inner = jax.random.fold_in(key, 11)
    base = jnp.clip(jax.random.normal(inner, (2, PROMPT, KV_HEADS * HEAD), jnp.float32), -4.0, 4.0)
    return base.astype(jnp.bfloat16)


def draw_queries(key, part):
    inner = jax.random.fold_in(key, 13)
    base = jnp.clip(3.0 * jax.random.normal(inner, (RESP, LEN, HEADS * HEAD), jnp.float32), -18.0, 18.0)
    return base.astype(jnp.bfloat16)


def draw_lengths(key, part):
    values = jax.random.randint(jax.random.fold_in(key, 3), (RESP,), LEN // 4, LEN + 1, dtype=jnp.int32)
    return values.at[0].set(LEN)


def steps_of(own_key, dims, split, smallest, top_value):
    def one(dim, shards_of):
        heights = jax.random.uniform(jax.random.fold_in(jax.random.fold_in(own_key, 6), dim), (shards_of,), jnp.float32, smallest / len(split), top_value / len(split))
        return jnp.repeat(jnp.exp(heights), dims[dim] // shards_of).reshape((-1,) + (1,) * (len(dims) - dim - 1))

    level = one(*split[0])
    for cut in split[1:]:
        level = level * one(*cut)
    return level


def noise(key, extent, deviation, reach, pieces=(), kind=jnp.bfloat16):
    values = jax.random.normal(key, extent, jnp.float32) * deviation
    if len(pieces) > 0:
        values = steps_of(key, extent, pieces, -0.22, 0.18) * values
    return jnp.clip(values, min=-reach, max=reach).astype(kind)


def setup_inputs(seed: int = 0) -> dict:
    key_of = jax.random.split(jax.random.key(seed), 5)
    return {
        "queries": draw_queries(jax.random.fold_in(key_of[4], 71), 0),
        "prompt_kv": draw_prompt_kv(jax.random.fold_in(key_of[4], 71), 0),
        "response_kv": noise(key_of[2], (2, RESP, LEN, KV_HEADS * HEAD), 1.0, 4.0, ((1, 8), (2, 16))),
        "lengths": draw_lengths(jax.random.fold_in(key_of[4], 71), 0),
    }


def reference(queries, prompt_kv, response_kv, lengths):
    resp_count, seq_len, width = queries.shape
    kv_width = prompt_kv.shape[2]
    kv_heads = kv_width // HEAD
    group_size = width // kv_width
    score_scale = 1.0 / math.sqrt(HEAD)
    prompt_keys = prompt_kv[0].astype(jnp.float32).reshape(PROMPT, kv_heads, HEAD)
    prompt_values = prompt_kv[1].astype(jnp.float32).reshape(PROMPT, kv_heads, HEAD)
    positions = jnp.arange(seq_len, dtype=jnp.int32)

    def one_response(operands):
        query_block, keys_resp, values_resp, length = operands
        query_heads = query_block.astype(jnp.float32).reshape(seq_len, kv_heads, group_size, HEAD)
        all_keys = jnp.concatenate([prompt_keys, keys_resp.astype(jnp.float32).reshape(seq_len, kv_heads, HEAD)], axis=0)
        all_values = jnp.concatenate([prompt_values, values_resp.astype(jnp.float32).reshape(seq_len, kv_heads, HEAD)], axis=0)
        scores = jnp.einsum('ikgd,jkd->ikgj', query_heads, all_keys, precision=lax.Precision.HIGHEST) * score_scale
        causal = (positions[None, :] <= positions[:, None]) & (positions[None, :] < length)
        is_live = jnp.concatenate([jnp.ones((seq_len, PROMPT), bool), causal], axis=1)[:, None, None, :]
        row_max = lax.optimization_barrier(jnp.max(jnp.where(is_live, scores, -1e+30), axis=-1))
        weights = jnp.where(is_live, jnp.exp(scores - row_max[..., None]), 0.0)
        total = lax.optimization_barrier(jnp.sum(weights, axis=-1))
        rounded = lax.optimization_barrier(weights.astype(jnp.bfloat16)).astype(jnp.float32)
        mixed = jnp.einsum('ikgj,jkd->ikgd', rounded, all_values, precision=lax.Precision.HIGHEST) / total[..., None]
        row_live = positions < length
        output = jnp.where(row_live[:, None, None, None], mixed, 0.0).reshape(seq_len, width).astype(jnp.bfloat16)
        log_total = jnp.where(row_live[:, None, None], row_max + jnp.log(total), 0.0).reshape(seq_len, kv_heads * group_size)
        return (output, log_total.astype(jnp.float32))
    attended, row_lse = lax.map(one_response, (queries, response_kv[0], response_kv[1], lengths))
    return (attended, row_lse)
```

```python
import functools
import math

import jax
import jax.numpy as jnp
from jax import lax
from jax.experimental import pallas as pl
from jax.experimental.pallas import tpu as pltpu
from jax.sharding import PartitionSpec as P

HEAD = 128
NEG = -1e30


def stack_groups(q, groups):
    return jnp.concatenate([q[:, g * HEAD:(g + 1) * HEAD] for g in range(groups)], axis=0)


def prompt_kernel(meta_ref, q_ref, k_ref, v_ref, acc_ref, ml_ref, *, rows, groups, scale):
    r = pl.program_id(0)
    c = meta_ref[meta_ref.shape[0] - 1]
    live_any = meta_ref[r] > rows * c

    @pl.when(live_any)
    def _():
        qk = stack_groups(q_ref[0], groups)
        keys = k_ref[0]
        s = lax.dot_general(qk, keys, (((1,), (1,)), ((), ())), preferred_element_type=jnp.float32) * scale
        m = jnp.max(s, axis=-1, keepdims=True)
        p = jnp.exp(s - m)
        l = jnp.sum(p, axis=-1, keepdims=True)
        acc_ref[0, 0] = jnp.dot(p.astype(jnp.bfloat16), v_ref[0], preferred_element_type=jnp.float32)
        lane = lax.broadcasted_iota(jnp.int32, (qk.shape[0], 128), 1)
        both = jnp.where(lane == 0, m, l)
        ml_ref[0, 0] = both.T[0:8]


def resp_kernel(meta_ref, q_ref, k_ref, v_ref, acc_ref, ml_ref, out_ref, lse_ref, *, rows, groups, scale, block):
    r = pl.program_id(0)
    c = meta_ref[meta_ref.shape[0] - 1]
    length = meta_ref[r]
    live_any = length > rows * c
    nrow = rows * groups

    @pl.when(jnp.logical_not(live_any))
    def _():
        out_ref[...] = jnp.zeros(out_ref.shape, out_ref.dtype)
        lse_ref[...] = jnp.zeros(lse_ref.shape, lse_ref.dtype)

    @pl.when(live_any)
    def _():
        qk = stack_groups(q_ref[0], groups)
        t = ml_ref[0, 0].T
        m0 = t[:, 0:1]
        l0 = t[:, 1:2]
        acc0 = acc_ref[0, 0]
        row_i = rows * c + lax.broadcasted_iota(jnp.int32, (nrow, 1), 0) % rows
        nkeys = jnp.minimum(rows * (c + 1), length)
        nblocks = (nkeys + block - 1) // block

        def body(kb, carry):
            m, l, acc = carry
            start = pl.multiple_of(kb * block, block)
            keys = k_ref[0, 0, pl.ds(start, block), :]
            vals = v_ref[0, 0, pl.ds(start, block), :]
            s = lax.dot_general(qk, keys, (((1,), (1,)), ((), ())), preferred_element_type=jnp.float32) * scale
            j = start + lax.broadcasted_iota(jnp.int32, (nrow, block), 1)
            live = (j <= row_i) & (j < length)
            s = jnp.where(live, s, NEG)
            m_new = jnp.maximum(m, jnp.max(s, axis=-1, keepdims=True))
            alpha = jnp.exp(m - m_new)
            p = jnp.where(live, jnp.exp(s - m_new), 0.0)
            l_new = alpha * l + jnp.sum(p, axis=-1, keepdims=True)
            acc_new = alpha * acc + jnp.dot(p.astype(jnp.bfloat16), vals, preferred_element_type=jnp.float32)
            return m_new, l_new, acc_new

        m, l, acc = lax.fori_loop(0, nblocks, body, (m0, l0, acc0))
        row_live = row_i < length
        o = jnp.where(row_live, acc / l, 0.0).astype(out_ref.dtype)
        for g in range(groups):
            out_ref[0, :, g * HEAD:(g + 1) * HEAD] = o[g * rows:(g + 1) * rows]
        lse = jnp.where(row_live, m + jnp.log(l), 0.0)
        lse_ref[0, 0] = jnp.broadcast_to(lse, (nrow, 128)).T[0:1]


def per_device(queries, prompt_kv, response_kv, lengths):
    resp_local, rows, width = queries.shape
    kv_width = prompt_kv.shape[2]
    kv_heads = kv_width // HEAD
    groups = width // kv_width
    nrow = rows * groups
    scale = 1.0 / math.sqrt(HEAD)
    c = lax.axis_index("ctx")
    meta = jnp.concatenate([lengths.astype(jnp.int32), c.astype(jnp.int32)[None]])

    full_prompt = lax.all_gather(lax.all_gather(prompt_kv, "ctx", axis=1, tiled=True), "resp", axis=1, tiled=True)
    full_resp = lax.all_gather(response_kv, "ctx", axis=2, tiled=True)
    n_prompt = full_prompt.shape[1]
    n_resp = full_resp.shape[2]

    grid = (resp_local, kv_heads)
    q_spec = pl.BlockSpec((1, rows, kv_width), lambda r, k, meta: (r, 0, k))
    acc_spec = pl.BlockSpec((1, 1, nrow, HEAD), lambda r, k, meta: (r, k, 0, 0))
    ml_spec = pl.BlockSpec((1, 1, 8, nrow), lambda r, k, meta: (r, k, 0, 0))
    acc, ml = pl.pallas_call(
        functools.partial(prompt_kernel, rows=rows, groups=groups, scale=scale),
        grid_spec=pltpu.PrefetchScalarGridSpec(
            num_scalar_prefetch=1,
            grid=grid,
            in_specs=[
                q_spec,
                pl.BlockSpec((1, n_prompt, HEAD), lambda r, k, meta: (0, 0, k)),
                pl.BlockSpec((1, n_prompt, HEAD), lambda r, k, meta: (1, 0, k)),
            ],
            out_specs=[acc_spec, ml_spec],
        ),
        out_shape=[
            jax.ShapeDtypeStruct((resp_local, kv_heads, nrow, HEAD), jnp.float32),
            jax.ShapeDtypeStruct((resp_local, kv_heads, 8, nrow), jnp.float32),
        ],
        cost_estimate=pl.CostEstimate(
            flops=4 * resp_local * kv_heads * nrow * n_prompt * HEAD,
            transcendentals=resp_local * kv_heads * nrow * n_prompt,
            bytes_accessed=2 * (queries.size + full_prompt.size) + 4 * resp_local * kv_heads * nrow * HEAD,
        ),
    )(meta, queries, full_prompt, full_prompt)

    block = 128
    attended, lse_t = pl.pallas_call(
        functools.partial(resp_kernel, rows=rows, groups=groups, scale=scale, block=block),
        grid_spec=pltpu.PrefetchScalarGridSpec(
            num_scalar_prefetch=1,
            grid=grid,
            in_specs=[
                q_spec,
                pl.BlockSpec((1, 1, n_resp, HEAD), lambda r, k, meta: (0, r, 0, k)),
                pl.BlockSpec((1, 1, n_resp, HEAD), lambda r, k, meta: (1, r, 0, k)),
                acc_spec,
                ml_spec,
            ],
            out_specs=[
                q_spec,
                pl.BlockSpec((1, 1, 1, nrow), lambda r, k, meta: (r, k, 0, 0)),
            ],
        ),
        out_shape=[
            jax.ShapeDtypeStruct(queries.shape, queries.dtype),
            jax.ShapeDtypeStruct((resp_local, kv_heads, 1, nrow), jnp.float32),
        ],
        cost_estimate=pl.CostEstimate(
            flops=4 * resp_local * kv_heads * nrow * n_resp * HEAD // 2,
            transcendentals=resp_local * kv_heads * nrow * n_resp // 2,
            bytes_accessed=2 * (2 * queries.size + full_resp.size) + 4 * resp_local * kv_heads * nrow * HEAD,
        ),
    )(meta, queries, full_resp, full_resp, acc, ml)

    row_lse = (
        lse_t.reshape(resp_local, kv_heads, groups, rows)
        .transpose(0, 3, 1, 2)
        .reshape(resp_local, rows, kv_heads * groups)
    )
    return attended, row_lse


def solution(mesh):
    placed = (
        P("resp", "ctx", None),
        P(None, ("resp", "ctx"), None),
        P(None, "resp", "ctx", None),
        P("resp"),
    )
    return jax.shard_map(
        per_device,
        mesh=mesh,
        in_specs=placed,
        out_specs=(P("resp", "ctx", None), P("resp", "ctx", None)),
        check_vma=False,
    )
```

```python
import functools
import math

import jax
import jax.numpy as jnp
from jax import lax
from jax.experimental import pallas as pl
from jax.experimental.pallas import tpu as pltpu
from jax.sharding import PartitionSpec as P

HEAD = 128
NEG = -1e30


def stack_groups(q, groups):
    return jnp.concatenate([q[:, g * HEAD:(g + 1) * HEAD] for g in range(groups)], axis=0)


def prompt_kernel(meta_ref, q_ref, k_ref, v_ref, acc_ref, ml_ref, *, rows, groups, scale):
    r = pl.program_id(1)
    c = meta_ref[meta_ref.shape[0] - 1]
    live_any = meta_ref[r] > rows * c

    @pl.when(live_any)
    def _():
        qk = stack_groups(q_ref[0], groups)
        keys = k_ref[0, 0]
        s = lax.dot_general(qk, keys, (((1,), (1,)), ((), ())), preferred_element_type=jnp.float32) * scale
        m = jnp.max(s, axis=-1, keepdims=True)
        p = jnp.exp(s - m)
        l = jnp.sum(p, axis=-1, keepdims=True)
        acc_ref[0, 0] = jnp.dot(p.astype(jnp.bfloat16), v_ref[0, 0], preferred_element_type=jnp.float32)
        lane = lax.broadcasted_iota(jnp.int32, (qk.shape[0], 128), 1)
        both = jnp.where(lane == 0, m, l)
        ml_ref[0, 0] = both.T[0:8]


def resp_kernel(meta_ref, q_ref, k_ref, v_ref, acc_ref, ml_ref, out_ref, lse_ref, *, rows, groups, scale, block):
    r = pl.program_id(0)
    c = meta_ref[meta_ref.shape[0] - 1]
    length = meta_ref[r]
    live_any = length > rows * c
    nrow = rows * groups

    @pl.when(jnp.logical_not(live_any))
    def _():
        out_ref[...] = jnp.zeros(out_ref.shape, out_ref.dtype)
        lse_ref[...] = jnp.zeros(lse_ref.shape, lse_ref.dtype)

    @pl.when(live_any)
    def _():
        qk = stack_groups(q_ref[0], groups)
        t = ml_ref[0, 0].T
        m0 = t[:, 0:1]
        l0 = t[:, 1:2]
        acc0 = acc_ref[0, 0]
        row_i = rows * c + lax.broadcasted_iota(jnp.int32, (nrow, 1), 0) % rows
        nkeys = jnp.minimum(rows * (c + 1), length)
        nblocks = (nkeys + block - 1) // block

        def body(kb, carry):
            m, l, acc = carry
            start = pl.multiple_of(kb * block, block)
            keys = k_ref[0, 0, 0, pl.ds(start, block), :]
            vals = v_ref[0, 0, 0, pl.ds(start, block), :]
            s = lax.dot_general(qk, keys, (((1,), (1,)), ((), ())), preferred_element_type=jnp.float32) * scale
            j = start + lax.broadcasted_iota(jnp.int32, (nrow, block), 1)
            live = (j <= row_i) & (j < length)
            s = jnp.where(live, s, NEG)
            m_new = jnp.maximum(m, jnp.max(s, axis=-1, keepdims=True))
            alpha = jnp.exp(m - m_new)
            p = jnp.where(live, jnp.exp(s - m_new), 0.0)
            l_new = alpha * l + jnp.sum(p, axis=-1, keepdims=True)
            acc_new = alpha * acc + jnp.dot(p.astype(jnp.bfloat16), vals, preferred_element_type=jnp.float32)
            return m_new, l_new, acc_new

        m, l, acc = lax.fori_loop(0, nblocks, body, (m0, l0, acc0))
        row_live = row_i < length
        o = jnp.where(row_live, acc / l, 0.0).astype(out_ref.dtype)
        for g in range(groups):
            out_ref[0, :, g * HEAD:(g + 1) * HEAD] = o[g * rows:(g + 1) * rows]
        lse = jnp.where(row_live, m + jnp.log(l), 0.0)
        lse_ref[0, 0] = jnp.broadcast_to(lse, (nrow, 128)).T[0:1]


def per_device(queries, prompt_kv, response_kv, lengths):
    resp_local, rows, width = queries.shape
    kv_width = prompt_kv.shape[2]
    kv_heads = kv_width // HEAD
    groups = width // kv_width
    nrow = rows * groups
    scale = 1.0 / math.sqrt(HEAD)
    c = lax.axis_index("ctx")
    meta = jnp.concatenate([lengths.astype(jnp.int32), c.astype(jnp.int32)[None]])

    own_prompt = prompt_kv.reshape(2, -1, kv_heads, HEAD).transpose(0, 2, 1, 3)
    full_prompt = lax.all_gather(lax.all_gather(own_prompt, "ctx", axis=2, tiled=True), "resp", axis=2, tiled=True)
    own_resp = response_kv.reshape(2, resp_local, rows, kv_heads, HEAD).transpose(0, 1, 3, 2, 4)
    full_resp = lax.all_gather(own_resp, "ctx", axis=3, tiled=True)
    n_prompt = full_prompt.shape[2]
    n_resp = full_resp.shape[3]

    grid = (resp_local, kv_heads)
    q_spec = pl.BlockSpec((1, rows, kv_width), lambda r, k, meta: (r, 0, k))
    acc_spec = pl.BlockSpec((1, 1, nrow, HEAD), lambda r, k, meta: (r, k, 0, 0))
    ml_spec = pl.BlockSpec((1, 1, 8, nrow), lambda r, k, meta: (r, k, 0, 0))
    q_spec_t = pl.BlockSpec((1, rows, kv_width), lambda k, r, meta: (r, 0, k))
    acc_spec_t = pl.BlockSpec((1, 1, nrow, HEAD), lambda k, r, meta: (r, k, 0, 0))
    ml_spec_t = pl.BlockSpec((1, 1, 8, nrow), lambda k, r, meta: (r, k, 0, 0))
    acc, ml = pl.pallas_call(
        functools.partial(prompt_kernel, rows=rows, groups=groups, scale=scale),
        grid_spec=pltpu.PrefetchScalarGridSpec(
            num_scalar_prefetch=1,
            grid=(kv_heads, resp_local),
            in_specs=[
                q_spec_t,
                pl.BlockSpec((1, 1, n_prompt, HEAD), lambda k, r, meta: (0, k, 0, 0)),
                pl.BlockSpec((1, 1, n_prompt, HEAD), lambda k, r, meta: (1, k, 0, 0)),
            ],
            out_specs=[acc_spec_t, ml_spec_t],
        ),
        out_shape=[
            jax.ShapeDtypeStruct((resp_local, kv_heads, nrow, HEAD), jnp.float32),
            jax.ShapeDtypeStruct((resp_local, kv_heads, 8, nrow), jnp.float32),
        ],
        cost_estimate=pl.CostEstimate(
            flops=4 * resp_local * kv_heads * nrow * n_prompt * HEAD,
            transcendentals=resp_local * kv_heads * nrow * n_prompt,
            bytes_accessed=2 * (queries.size + full_prompt.size) + 4 * resp_local * kv_heads * nrow * HEAD,
        ),
    )(meta, queries, full_prompt, full_prompt)

    block = 128
    attended, lse_t = pl.pallas_call(
        functools.partial(resp_kernel, rows=rows, groups=groups, scale=scale, block=block),
        grid_spec=pltpu.PrefetchScalarGridSpec(
            num_scalar_prefetch=1,
            grid=grid,
            in_specs=[
                q_spec,
                pl.BlockSpec((1, 1, 1, n_resp, HEAD), lambda r, k, meta: (0, r, k, 0, 0)),
                pl.BlockSpec((1, 1, 1, n_resp, HEAD), lambda r, k, meta: (1, r, k, 0, 0)),
                acc_spec,
                ml_spec,
            ],
            out_specs=[
                q_spec,
                pl.BlockSpec((1, 1, 1, nrow), lambda r, k, meta: (r, k, 0, 0)),
            ],
        ),
        out_shape=[
            jax.ShapeDtypeStruct(queries.shape, queries.dtype),
            jax.ShapeDtypeStruct((resp_local, kv_heads, 1, nrow), jnp.float32),
        ],
        cost_estimate=pl.CostEstimate(
            flops=4 * resp_local * kv_heads * nrow * n_resp * HEAD // 2,
            transcendentals=resp_local * kv_heads * nrow * n_resp // 2,
            bytes_accessed=2 * (2 * queries.size + full_resp.size) + 4 * resp_local * kv_heads * nrow * HEAD,
        ),
    )(meta, queries, full_resp, full_resp, acc, ml)

    row_lse = (
        lse_t.reshape(resp_local, kv_heads, groups, rows)
        .transpose(0, 3, 1, 2)
        .reshape(resp_local, rows, kv_heads * groups)
    )
    return attended, row_lse


def solution(mesh):
    placed = (
        P("resp", "ctx", None),
        P(None, ("resp", "ctx"), None),
        P(None, "resp", "ctx", None),
        P("resp"),
    )
    return jax.shard_map(
        per_device,
        mesh=mesh,
        in_specs=placed,
        out_specs=(P("resp", "ctx", None), P("resp", "ctx", None)),
        check_vma=False,
    )
```

```python
import functools
import math

import jax
import jax.numpy as jnp
from jax import lax
from jax.experimental import pallas as pl
from jax.experimental.pallas import tpu as pltpu
from jax.sharding import PartitionSpec as P

HEAD = 128
NEG = -1e30


def stack_groups(q, groups):
    return jnp.concatenate([q[:, g * HEAD:(g + 1) * HEAD] for g in range(groups)], axis=0)


def scores(qk, keys, scale):
    return lax.dot_general(qk, keys, (((1,), (1,)), ((), ())), preferred_element_type=jnp.float32) * scale


def prompt_kernel(meta_ref, q_ref, pk_ref, own_ref, acc_ref, ml_ref, *, rows, groups, kv_heads, scale):
    r = pl.program_id(0)
    c = meta_ref[meta_ref.shape[0] - 1]
    length = meta_ref[r]
    nrow = rows * groups
    kv_width = groups * HEAD

    @pl.when(length > rows * c)
    def _():
        row_i = rows * c + lax.broadcasted_iota(jnp.int32, (nrow, 1), 0) % rows
        j = rows * c + lax.broadcasted_iota(jnp.int32, (nrow, rows), 1)
        live = (j <= row_i) & (j < length)
        lane = lax.broadcasted_iota(jnp.int32, (nrow, 128), 1)

        def head(k, carry):
            col = pl.multiple_of(k * HEAD, HEAD)
            qk = stack_groups(q_ref[0, :, pl.ds(pl.multiple_of(k * kv_width, kv_width), kv_width)], groups)
            s1 = scores(qk, pk_ref[0, :, pl.ds(col, HEAD)], scale)
            s2 = jnp.where(live, scores(qk, own_ref[0, 0, :, pl.ds(col, HEAD)], scale), NEG)
            m = jnp.maximum(jnp.max(s1, axis=-1, keepdims=True), jnp.max(s2, axis=-1, keepdims=True))
            p1 = jnp.exp(s1 - m)
            p2 = jnp.where(live, jnp.exp(s2 - m), 0.0)
            l = jnp.sum(p1, axis=-1, keepdims=True) + jnp.sum(p2, axis=-1, keepdims=True)
            acc = jnp.dot(p1.astype(jnp.bfloat16), pk_ref[1, :, pl.ds(col, HEAD)], preferred_element_type=jnp.float32)
            acc = acc + jnp.dot(p2.astype(jnp.bfloat16), own_ref[1, 0, :, pl.ds(col, HEAD)], preferred_element_type=jnp.float32)
            acc_ref[0, k] = acc
            ml_ref[0, k] = jnp.where(lane == 0, m, l).T[0:8]
            return carry

        lax.fori_loop(0, kv_heads, head, 0)


def resp_kernel(meta_ref, q_ref, rk_ref, acc_ref, ml_ref, out_ref, lse_ref, *, rows, groups, kv_heads, scale, block):
    r = pl.program_id(0)
    c = meta_ref[meta_ref.shape[0] - 1]
    length = meta_ref[r]
    live_any = length > rows * c
    nrow = rows * groups
    kv_width = groups * HEAD

    @pl.when(jnp.logical_not(live_any))
    def _():
        out_ref[...] = jnp.zeros(out_ref.shape, out_ref.dtype)
        lse_ref[...] = jnp.zeros(lse_ref.shape, lse_ref.dtype)

    @pl.when(live_any)
    def _():
        row_i = rows * c + lax.broadcasted_iota(jnp.int32, (nrow, 1), 0) % rows
        row_live = row_i < length
        limit = jnp.minimum(rows * c, length)
        nblocks = (limit + block - 1) // block

        def head(k, carry):
            col = pl.multiple_of(k * HEAD, HEAD)
            qoff = pl.multiple_of(k * kv_width, kv_width)
            qk = stack_groups(q_ref[0, :, pl.ds(qoff, kv_width)], groups)
            t = ml_ref[0, k].T
            m0 = t[:, 0:1]
            l0 = t[:, 1:2]

            def body(kb, state):
                m, l, acc = state
                start = pl.multiple_of(kb * block, block)
                s = scores(qk, rk_ref[0, 0, pl.ds(start, block), pl.ds(col, HEAD)], scale)
                j = start + lax.broadcasted_iota(jnp.int32, (nrow, block), 1)
                live = j < limit
                s = jnp.where(live, s, NEG)
                m_new = jnp.maximum(m, jnp.max(s, axis=-1, keepdims=True))
                alpha = jnp.exp(m - m_new)
                p = jnp.where(live, jnp.exp(s - m_new), 0.0)
                l_new = alpha * l + jnp.sum(p, axis=-1, keepdims=True)
                pv = jnp.dot(p.astype(jnp.bfloat16), rk_ref[1, 0, pl.ds(start, block), pl.ds(col, HEAD)],
                             preferred_element_type=jnp.float32)
                return m_new, l_new, alpha * acc + pv

            m, l, acc = lax.fori_loop(0, nblocks, body, (m0, l0, acc_ref[0, k]))
            o = jnp.where(row_live, acc / l, 0.0).astype(out_ref.dtype)
            for g in range(groups):
                out_ref[0, :, pl.ds(qoff + g * HEAD, HEAD)] = o[g * rows:(g + 1) * rows]
            lse = jnp.where(row_live, m + jnp.log(l), 0.0)
            lse_ref[0, k] = jnp.broadcast_to(lse, (nrow, 128)).T[0:1]
            return carry

        lax.fori_loop(0, kv_heads, head, 0)


def per_device(queries, prompt_kv, response_kv, lengths):
    resp_local, rows, width = queries.shape
    kv_width = prompt_kv.shape[2]
    kv_heads = kv_width // HEAD
    groups = width // kv_width
    nrow = rows * groups
    scale = 1.0 / math.sqrt(HEAD)
    c = lax.axis_index("ctx")
    meta = jnp.concatenate([lengths.astype(jnp.int32), c.astype(jnp.int32)[None]])

    full_prompt = lax.all_gather(lax.all_gather(prompt_kv, "ctx", axis=1, tiled=True), "resp", axis=1, tiled=True)
    full_resp = lax.all_gather(response_kv, "ctx", axis=2, tiled=True)
    n_prompt = full_prompt.shape[1]
    n_resp = full_resp.shape[2]

    q_spec = pl.BlockSpec((1, rows, width), lambda r, meta: (r, 0, 0))
    acc_spec = pl.BlockSpec((1, kv_heads, nrow, HEAD), lambda r, meta: (r, 0, 0, 0))
    ml_spec = pl.BlockSpec((1, kv_heads, 8, nrow), lambda r, meta: (r, 0, 0, 0))
    params = pltpu.CompilerParams(vmem_limit_bytes=48 * 1024 * 1024)
    acc, ml = pl.pallas_call(
        functools.partial(prompt_kernel, rows=rows, groups=groups, kv_heads=kv_heads, scale=scale),
        grid_spec=pltpu.PrefetchScalarGridSpec(
            num_scalar_prefetch=1,
            grid=(resp_local,),
            in_specs=[
                q_spec,
                pl.BlockSpec((2, n_prompt, kv_width), lambda r, meta: (0, 0, 0)),
                pl.BlockSpec((2, 1, rows, kv_width), lambda r, meta: (0, r, 0, 0)),
            ],
            out_specs=[acc_spec, ml_spec],
        ),
        out_shape=[
            jax.ShapeDtypeStruct((resp_local, kv_heads, nrow, HEAD), jnp.float32),
            jax.ShapeDtypeStruct((resp_local, kv_heads, 8, nrow), jnp.float32),
        ],
        compiler_params=params,
        cost_estimate=pl.CostEstimate(
            flops=4 * resp_local * kv_heads * nrow * (n_prompt + rows) * HEAD,
            transcendentals=resp_local * kv_heads * nrow * (n_prompt + rows),
            bytes_accessed=2 * (queries.size + full_prompt.size) + 4 * resp_local * kv_heads * nrow * HEAD,
        ),
    )(meta, queries, full_prompt, response_kv)

    block = 128
    attended, lse_t = pl.pallas_call(
        functools.partial(resp_kernel, rows=rows, groups=groups, kv_heads=kv_heads, scale=scale, block=block),
        grid_spec=pltpu.PrefetchScalarGridSpec(
            num_scalar_prefetch=1,
            grid=(resp_local,),
            in_specs=[
                q_spec,
                pl.BlockSpec((2, 1, n_resp, kv_width), lambda r, meta: (0, r, 0, 0)),
                acc_spec,
                ml_spec,
            ],
            out_specs=[
                q_spec,
                pl.BlockSpec((1, kv_heads, 1, nrow), lambda r, meta: (r, 0, 0, 0)),
            ],
        ),
        out_shape=[
            jax.ShapeDtypeStruct(queries.shape, queries.dtype),
            jax.ShapeDtypeStruct((resp_local, kv_heads, 1, nrow), jnp.float32),
        ],
        compiler_params=params,
        cost_estimate=pl.CostEstimate(
            flops=4 * resp_local * kv_heads * nrow * n_resp * HEAD // 2,
            transcendentals=resp_local * kv_heads * nrow * n_resp // 2,
            bytes_accessed=2 * (2 * queries.size + full_resp.size) + 4 * resp_local * kv_heads * nrow * HEAD,
        ),
    )(meta, queries, full_resp, acc, ml)

    row_lse = (
        lse_t.reshape(resp_local, kv_heads, groups, rows)
        .transpose(0, 3, 1, 2)
        .reshape(resp_local, rows, kv_heads * groups)
    )
    return attended, row_lse


def solution(mesh):
    placed = (
        P("resp", "ctx", None),
        P(None, ("resp", "ctx"), None),
        P(None, "resp", "ctx", None),
        P("resp"),
    )
    return jax.shard_map(
        per_device,
        mesh=mesh,
        in_specs=placed,
        out_specs=(P("resp", "ctx", None), P("resp", "ctx", None)),
        check_vma=False,
    )
```

```python
import functools
import math

import jax
import jax.numpy as jnp
from jax import lax
from jax.experimental import pallas as pl
from jax.experimental.pallas import tpu as pltpu
from jax.sharding import PartitionSpec as P

HEAD = 128
NEG = -1e30


def stack_groups(q, groups):
    return jnp.concatenate([q[:, g * HEAD:(g + 1) * HEAD] for g in range(groups)], axis=0)


def scores(qk, keys, scale):
    return lax.dot_general(qk, keys, (((1,), (1,)), ((), ())), preferred_element_type=jnp.float32) * scale


def prompt_kernel(meta_ref, q_ref, pk_ref, own_ref, acc_ref, ml_ref, *, rows, groups, kv_heads, scale):
    r = pl.program_id(0)
    c = meta_ref[meta_ref.shape[0] - 1]
    length = meta_ref[r]
    nrow = rows * groups
    kv_width = groups * HEAD

    @pl.when(length > rows * c)
    def _():
        row_i = rows * c + lax.broadcasted_iota(jnp.int32, (nrow, 1), 0) % rows
        j = rows * c + lax.broadcasted_iota(jnp.int32, (nrow, rows), 1)
        live = (j <= row_i) & (j < length)
        lane = lax.broadcasted_iota(jnp.int32, (nrow, 128), 1)

        def head(k, carry):
            col = pl.multiple_of(k * HEAD, HEAD)
            qk = stack_groups(q_ref[0, :, pl.ds(pl.multiple_of(k * kv_width, kv_width), kv_width)], groups)
            s1 = scores(qk, pk_ref[0, :, pl.ds(col, HEAD)], scale)
            s2 = jnp.where(live, scores(qk, own_ref[0, 0, :, pl.ds(col, HEAD)], scale), NEG)
            m = jnp.maximum(jnp.max(s1, axis=-1, keepdims=True), jnp.max(s2, axis=-1, keepdims=True))
            p1 = jnp.exp(s1 - m)
            p2 = jnp.where(live, jnp.exp(s2 - m), 0.0)
            l = jnp.sum(p1, axis=-1, keepdims=True) + jnp.sum(p2, axis=-1, keepdims=True)
            acc = jnp.dot(p1.astype(jnp.bfloat16), pk_ref[1, :, pl.ds(col, HEAD)], preferred_element_type=jnp.float32)
            acc = acc + jnp.dot(p2.astype(jnp.bfloat16), own_ref[1, 0, :, pl.ds(col, HEAD)], preferred_element_type=jnp.float32)
            acc_ref[0, k] = acc
            ml_ref[0, k] = jnp.where(lane == 0, m, l).T[0:8]
            return carry

        lax.fori_loop(0, kv_heads, head, 0)


def resp_kernel(meta_ref, q_ref, rk_hbm, acc_ref, ml_ref, out_ref, lse_ref, kv_buf, sems,
                *, rows, groups, kv_heads, scale, block, max_blocks):
    r = pl.program_id(0)
    c = meta_ref[meta_ref.shape[0] - 1]
    length = meta_ref[r]
    live_any = length > rows * c
    nrow = rows * groups
    kv_width = groups * HEAD
    limit = jnp.minimum(rows * c, length)
    nblocks = (limit + block - 1) // block

    @pl.when(jnp.logical_not(live_any))
    def _():
        out_ref[...] = jnp.zeros(out_ref.shape, out_ref.dtype)
        lse_ref[...] = jnp.zeros(lse_ref.shape, lse_ref.dtype)

    def run(n):
        width = n * block
        if n > 0:
            copies = [
                pltpu.make_async_copy(rk_hbm.at[h, r, pl.ds(0, width), :], kv_buf.at[h, pl.ds(0, width), :], sems.at[h])
                for h in range(2)
            ]
            for cp in copies:
                cp.start()
            for cp in copies:
                cp.wait()
        row_i = rows * c + lax.broadcasted_iota(jnp.int32, (nrow, 1), 0) % rows
        row_live = row_i < length

        def head(k, carry):
            col = pl.multiple_of(k * HEAD, HEAD)
            qoff = pl.multiple_of(k * kv_width, kv_width)
            t = ml_ref[0, k].T
            m = t[:, 0:1]
            l = t[:, 1:2]
            acc = acc_ref[0, k]
            if n > 0:
                qk = stack_groups(q_ref[0, :, pl.ds(qoff, kv_width)], groups)
                s = scores(qk, kv_buf[0, 0:width, pl.ds(col, HEAD)], scale)
                live = lax.broadcasted_iota(jnp.int32, (nrow, width), 1) < limit
                s = jnp.where(live, s, NEG)
                m_new = jnp.maximum(m, jnp.max(s, axis=-1, keepdims=True))
                alpha = jnp.exp(m - m_new)
                p = jnp.where(live, jnp.exp(s - m_new), 0.0)
                l = alpha * l + jnp.sum(p, axis=-1, keepdims=True)
                pv = jnp.dot(p.astype(jnp.bfloat16), kv_buf[1, 0:width, pl.ds(col, HEAD)],
                             preferred_element_type=jnp.float32)
                acc = alpha * acc + pv
                m = m_new
            o = jnp.where(row_live, acc / l, 0.0).astype(out_ref.dtype)
            for g in range(groups):
                out_ref[0, :, pl.ds(qoff + g * HEAD, HEAD)] = o[g * rows:(g + 1) * rows]
            lse = jnp.where(row_live, m + jnp.log(l), 0.0)
            lse_ref[0, k] = jnp.broadcast_to(lse, (nrow, 128)).T[0:1]
            return carry

        lax.fori_loop(0, kv_heads, head, 0)

    for n in range(max_blocks + 1):
        pl.when(live_any & (nblocks == n))(functools.partial(run, n))


def per_device(queries, prompt_kv, response_kv, lengths):
    resp_local, rows, width = queries.shape
    kv_width = prompt_kv.shape[2]
    kv_heads = kv_width // HEAD
    groups = width // kv_width
    nrow = rows * groups
    scale = 1.0 / math.sqrt(HEAD)
    c = lax.axis_index("ctx")
    meta = jnp.concatenate([lengths.astype(jnp.int32), c.astype(jnp.int32)[None]])

    full_prompt = lax.all_gather(lax.all_gather(prompt_kv, "ctx", axis=1, tiled=True), "resp", axis=1, tiled=True)
    full_resp = lax.all_gather(response_kv, "ctx", axis=2, tiled=True)
    n_prompt = full_prompt.shape[1]
    n_resp = full_resp.shape[2]

    q_spec = pl.BlockSpec((1, rows, width), lambda r, meta: (r, 0, 0))
    acc_spec = pl.BlockSpec((1, kv_heads, nrow, HEAD), lambda r, meta: (r, 0, 0, 0))
    ml_spec = pl.BlockSpec((1, kv_heads, 8, nrow), lambda r, meta: (r, 0, 0, 0))
    params = pltpu.CompilerParams(vmem_limit_bytes=48 * 1024 * 1024)
    acc, ml = pl.pallas_call(
        functools.partial(prompt_kernel, rows=rows, groups=groups, kv_heads=kv_heads, scale=scale),
        grid_spec=pltpu.PrefetchScalarGridSpec(
            num_scalar_prefetch=1,
            grid=(resp_local,),
            in_specs=[
                q_spec,
                pl.BlockSpec((2, n_prompt, kv_width), lambda r, meta: (0, 0, 0)),
                pl.BlockSpec((2, 1, rows, kv_width), lambda r, meta: (0, r, 0, 0)),
            ],
            out_specs=[acc_spec, ml_spec],
        ),
        out_shape=[
            jax.ShapeDtypeStruct((resp_local, kv_heads, nrow, HEAD), jnp.float32),
            jax.ShapeDtypeStruct((resp_local, kv_heads, 8, nrow), jnp.float32),
        ],
        compiler_params=params,
        cost_estimate=pl.CostEstimate(
            flops=4 * resp_local * kv_heads * nrow * (n_prompt + rows) * HEAD,
            transcendentals=resp_local * kv_heads * nrow * (n_prompt + rows),
            bytes_accessed=2 * (queries.size + full_prompt.size) + 4 * resp_local * kv_heads * nrow * HEAD,
        ),
    )(meta, queries, full_prompt, response_kv)

    block = 128
    max_blocks = (n_resp - rows + block - 1) // block
    attended, lse_t = pl.pallas_call(
        functools.partial(resp_kernel, rows=rows, groups=groups, kv_heads=kv_heads, scale=scale, block=block,
                          max_blocks=max_blocks),
        grid_spec=pltpu.PrefetchScalarGridSpec(
            num_scalar_prefetch=1,
            grid=(resp_local,),
            in_specs=[
                q_spec,
                pl.BlockSpec(memory_space=pl.ANY),
                acc_spec,
                ml_spec,
            ],
            out_specs=[
                q_spec,
                pl.BlockSpec((1, kv_heads, 1, nrow), lambda r, meta: (r, 0, 0, 0)),
            ],
            scratch_shapes=[
                pltpu.VMEM((2, max_blocks * block, kv_width), jnp.bfloat16),
                pltpu.SemaphoreType.DMA((2,)),
            ],
        ),
        out_shape=[
            jax.ShapeDtypeStruct(queries.shape, queries.dtype),
            jax.ShapeDtypeStruct((resp_local, kv_heads, 1, nrow), jnp.float32),
        ],
        compiler_params=params,
        cost_estimate=pl.CostEstimate(
            flops=4 * resp_local * kv_heads * nrow * n_resp * HEAD // 2,
            transcendentals=resp_local * kv_heads * nrow * n_resp // 2,
            bytes_accessed=2 * (2 * queries.size + full_resp.size) + 4 * resp_local * kv_heads * nrow * HEAD,
        ),
    )(meta, queries, full_resp, acc, ml)

    row_lse = (
        lse_t.reshape(resp_local, kv_heads, groups, rows)
        .transpose(0, 3, 1, 2)
        .reshape(resp_local, rows, kv_heads * groups)
    )
    return attended, row_lse


def solution(mesh):
    placed = (
        P("resp", "ctx", None),
        P(None, ("resp", "ctx"), None),
        P(None, "resp", "ctx", None),
        P("resp"),
    )
    return jax.shard_map(
        per_device,
        mesh=mesh,
        in_specs=placed,
        out_specs=(P("resp", "ctx", None), P("resp", "ctx", None)),
        check_vma=False,
    )
```

```python
import functools
import math

import jax
import jax.numpy as jnp
from jax import lax
from jax.experimental import pallas as pl
from jax.experimental.pallas import tpu as pltpu
from jax.sharding import PartitionSpec as P

HEAD = 128
NEG = -1e30


def stack_groups(q, groups):
    return jnp.concatenate([q[:, g * HEAD:(g + 1) * HEAD] for g in range(groups)], axis=0)


def scores(qk, keys, scale):
    return lax.dot_general(qk, keys, (((1,), (1,)), ((), ())), preferred_element_type=jnp.float32) * scale


def prompt_kernel(meta_ref, q_ref, pk_ref, own_ref, acc_ref, m_ref, l_ref, *, rows, groups, kv_heads, scale):
    r = pl.program_id(0)
    c = meta_ref[meta_ref.shape[0] - 1]
    length = meta_ref[r]
    nrow = rows * groups
    kv_width = groups * HEAD

    @pl.when(length > rows * c)
    def _():
        row_i = rows * c + lax.broadcasted_iota(jnp.int32, (nrow, 1), 0) % rows
        j = rows * c + lax.broadcasted_iota(jnp.int32, (nrow, rows), 1)
        live = (j <= row_i) & (j < length)

        def head(k, carry):
            col = pl.multiple_of(k * HEAD, HEAD)
            qk = stack_groups(q_ref[0, :, pl.ds(pl.multiple_of(k * kv_width, kv_width), kv_width)], groups)
            s1 = scores(qk, pk_ref[0, :, pl.ds(col, HEAD)], scale)
            s2 = jnp.where(live, scores(qk, own_ref[0, 0, :, pl.ds(col, HEAD)], scale), NEG)
            m = jnp.maximum(jnp.max(s1, axis=-1, keepdims=True), jnp.max(s2, axis=-1, keepdims=True))
            p1 = jnp.exp(s1 - m)
            p2 = jnp.where(live, jnp.exp(s2 - m), 0.0)
            l = jnp.sum(p1, axis=-1, keepdims=True) + jnp.sum(p2, axis=-1, keepdims=True)
            acc = jnp.dot(p1.astype(jnp.bfloat16), pk_ref[1, :, pl.ds(col, HEAD)], preferred_element_type=jnp.float32)
            acc = acc + jnp.dot(p2.astype(jnp.bfloat16), own_ref[1, 0, :, pl.ds(col, HEAD)], preferred_element_type=jnp.float32)
            acc_ref[0, k] = acc
            m_ref[0, k] = jnp.broadcast_to(m, (nrow, HEAD))
            l_ref[0, k] = jnp.broadcast_to(l, (nrow, HEAD))
            return carry

        lax.fori_loop(0, kv_heads, head, 0)


def resp_kernel(meta_ref, q_ref, rk_hbm, acc_ref, m_ref, l_ref, out_ref, lse_ref, kv_buf, sems,
                *, rows, groups, kv_heads, scale, block, max_blocks):
    r = pl.program_id(0)
    c = meta_ref[meta_ref.shape[0] - 1]
    length = meta_ref[r]
    live_any = length > rows * c
    nrow = rows * groups
    kv_width = groups * HEAD
    limit = jnp.minimum(rows * c, length)
    nblocks = (limit + block - 1) // block

    @pl.when(jnp.logical_not(live_any))
    def _():
        out_ref[...] = jnp.zeros(out_ref.shape, out_ref.dtype)
        lse_ref[...] = jnp.zeros(lse_ref.shape, lse_ref.dtype)

    def run(n):
        width = n * block
        if n > 0:
            copies = [
                pltpu.make_async_copy(rk_hbm.at[h, r, pl.ds(0, width), :], kv_buf.at[h, pl.ds(0, width), :], sems.at[h])
                for h in range(2)
            ]
            for cp in copies:
                cp.start()
            for cp in copies:
                cp.wait()
        row_i = rows * c + lax.broadcasted_iota(jnp.int32, (nrow, 1), 0) % rows
        row_live = row_i < length

        def head(k, carry):
            col = pl.multiple_of(k * HEAD, HEAD)
            qoff = pl.multiple_of(k * kv_width, kv_width)
            m = m_ref[0, k]
            l = l_ref[0, k]
            acc = acc_ref[0, k]
            if n > 0:
                qk = stack_groups(q_ref[0, :, pl.ds(qoff, kv_width)], groups)
                s = scores(qk, kv_buf[0, 0:width, pl.ds(col, HEAD)], scale)
                live = lax.broadcasted_iota(jnp.int32, (nrow, width), 1) < limit
                s = jnp.where(live, s, NEG)
                m_new = jnp.maximum(m, jnp.max(s, axis=-1, keepdims=True))
                alpha = jnp.exp(m - m_new)
                m_wide = m_new if n == 1 else jnp.concatenate([m_new] * n, axis=1)
                p = jnp.where(live, jnp.exp(s - m_wide), 0.0)
                l = alpha * l + jnp.sum(p, axis=-1, keepdims=True)
                pv = jnp.dot(p.astype(jnp.bfloat16), kv_buf[1, 0:width, pl.ds(col, HEAD)],
                             preferred_element_type=jnp.float32)
                acc = alpha * acc + pv
                m = m_new
            o = jnp.where(row_live, acc / l, 0.0).astype(out_ref.dtype)
            for g in range(groups):
                out_ref[0, :, pl.ds(qoff + g * HEAD, HEAD)] = o[g * rows:(g + 1) * rows]
            lse = jnp.where(row_live, m + jnp.log(l), 0.0)
            lse_ref[0, k] = lse.T[0:1]
            return carry

        lax.fori_loop(0, kv_heads, head, 0)

    for n in range(max_blocks + 1):
        pl.when(live_any & (nblocks == n))(functools.partial(run, n))


def per_device(queries, prompt_kv, response_kv, lengths):
    resp_local, rows, width = queries.shape
    kv_width = prompt_kv.shape[2]
    kv_heads = kv_width // HEAD
    groups = width // kv_width
    nrow = rows * groups
    scale = 1.0 / math.sqrt(HEAD)
    c = lax.axis_index("ctx")
    meta = jnp.concatenate([lengths.astype(jnp.int32), c.astype(jnp.int32)[None]])

    full_prompt = lax.all_gather(lax.all_gather(prompt_kv, "ctx", axis=1, tiled=True), "resp", axis=1, tiled=True)
    full_resp = lax.all_gather(response_kv, "ctx", axis=2, tiled=True)
    n_prompt = full_prompt.shape[1]
    n_resp = full_resp.shape[2]

    q_spec = pl.BlockSpec((1, rows, width), lambda r, meta: (r, 0, 0))
    acc_spec = pl.BlockSpec((1, kv_heads, nrow, HEAD), lambda r, meta: (r, 0, 0, 0))

    params = pltpu.CompilerParams(vmem_limit_bytes=48 * 1024 * 1024)
    acc, m_rep, l_rep = pl.pallas_call(
        functools.partial(prompt_kernel, rows=rows, groups=groups, kv_heads=kv_heads, scale=scale),
        grid_spec=pltpu.PrefetchScalarGridSpec(
            num_scalar_prefetch=1,
            grid=(resp_local,),
            in_specs=[
                q_spec,
                pl.BlockSpec((2, n_prompt, kv_width), lambda r, meta: (0, 0, 0)),
                pl.BlockSpec((2, 1, rows, kv_width), lambda r, meta: (0, r, 0, 0)),
            ],
            out_specs=[acc_spec, acc_spec, acc_spec],
        ),
        out_shape=[
            jax.ShapeDtypeStruct((resp_local, kv_heads, nrow, HEAD), jnp.float32),
            jax.ShapeDtypeStruct((resp_local, kv_heads, nrow, HEAD), jnp.float32),
            jax.ShapeDtypeStruct((resp_local, kv_heads, nrow, HEAD), jnp.float32),
        ],
        compiler_params=params,
        cost_estimate=pl.CostEstimate(
            flops=4 * resp_local * kv_heads * nrow * (n_prompt + rows) * HEAD,
            transcendentals=resp_local * kv_heads * nrow * (n_prompt + rows),
            bytes_accessed=2 * (queries.size + full_prompt.size) + 4 * resp_local * kv_heads * nrow * HEAD,
        ),
    )(meta, queries, full_prompt, response_kv)

    block = 128
    max_blocks = (n_resp - rows + block - 1) // block
    attended, lse_t = pl.pallas_call(
        functools.partial(resp_kernel, rows=rows, groups=groups, kv_heads=kv_heads, scale=scale, block=block,
                          max_blocks=max_blocks),
        grid_spec=pltpu.PrefetchScalarGridSpec(
            num_scalar_prefetch=1,
            grid=(resp_local,),
            in_specs=[
                q_spec,
                pl.BlockSpec(memory_space=pl.ANY),
                acc_spec,
                acc_spec,
                acc_spec,
            ],
            out_specs=[
                q_spec,
                pl.BlockSpec((1, kv_heads, 1, nrow), lambda r, meta: (r, 0, 0, 0)),
            ],
            scratch_shapes=[
                pltpu.VMEM((2, max_blocks * block, kv_width), jnp.bfloat16),
                pltpu.SemaphoreType.DMA((2,)),
            ],
        ),
        out_shape=[
            jax.ShapeDtypeStruct(queries.shape, queries.dtype),
            jax.ShapeDtypeStruct((resp_local, kv_heads, 1, nrow), jnp.float32),
        ],
        compiler_params=params,
        cost_estimate=pl.CostEstimate(
            flops=4 * resp_local * kv_heads * nrow * n_resp * HEAD // 2,
            transcendentals=resp_local * kv_heads * nrow * n_resp // 2,
            bytes_accessed=2 * (2 * queries.size + full_resp.size) + 4 * resp_local * kv_heads * nrow * HEAD,
        ),
    )(meta, queries, full_resp, acc, m_rep, l_rep)

    row_lse = (
        lse_t.reshape(resp_local, kv_heads, groups, rows)
        .transpose(0, 3, 1, 2)
        .reshape(resp_local, rows, kv_heads * groups)
    )
    return attended, row_lse


def solution(mesh):
    placed = (
        P("resp", "ctx", None),
        P(None, ("resp", "ctx"), None),
        P(None, "resp", "ctx", None),
        P("resp"),
    )
    return jax.shard_map(
        per_device,
        mesh=mesh,
        in_specs=placed,
        out_specs=(P("resp", "ctx", None), P("resp", "ctx", None)),
        check_vma=False,
    )
```

```python
import functools
import math

import jax
import jax.numpy as jnp
from jax import lax
from jax.experimental import pallas as pl
from jax.experimental.pallas import tpu as pltpu
from jax.sharding import PartitionSpec as P

HEAD = 128
NEG = -1e30


def stack_groups(q, groups):
    return jnp.concatenate([q[:, g * HEAD:(g + 1) * HEAD] for g in range(groups)], axis=0)


def scores(qk, keys, scale):
    return lax.dot_general(qk, keys, (((1,), (1,)), ((), ())), preferred_element_type=jnp.float32) * scale


def prompt_kernel(meta_ref, q_ref, *refs, rows, groups, kv_heads, scale, pieces):
    piece_refs = refs[:pieces]
    own_ref, acc_ref, m_ref, l_ref = refs[pieces:]
    r = pl.program_id(0)
    c = meta_ref[meta_ref.shape[0] - 1]
    length = meta_ref[r]
    nrow = rows * groups
    kv_width = groups * HEAD

    @pl.when(length > rows * c)
    def _():
        row_i = rows * c + lax.broadcasted_iota(jnp.int32, (nrow, 1), 0) % rows
        j = rows * c + lax.broadcasted_iota(jnp.int32, (nrow, rows), 1)
        live = (j <= row_i) & (j < length)

        def head(k, carry):
            col = pl.multiple_of(k * HEAD, HEAD)
            qk = stack_groups(q_ref[0, :, pl.ds(pl.multiple_of(k * kv_width, kv_width), kv_width)], groups)
            s1 = jnp.concatenate([scores(qk, p_ref[0, :, pl.ds(col, HEAD)], scale) for p_ref in piece_refs], axis=1)
            s2 = jnp.where(live, scores(qk, own_ref[0, 0, :, pl.ds(col, HEAD)], scale), NEG)
            m = jnp.maximum(jnp.max(s1, axis=-1, keepdims=True), jnp.max(s2, axis=-1, keepdims=True))
            p1 = jnp.exp(s1 - m)
            p2 = jnp.where(live, jnp.exp(s2 - m), 0.0)
            l = jnp.sum(p1, axis=-1, keepdims=True) + jnp.sum(p2, axis=-1, keepdims=True)
            p1 = p1.astype(jnp.bfloat16)
            width = p1.shape[1] // pieces
            acc = jnp.dot(p2.astype(jnp.bfloat16), own_ref[1, 0, :, pl.ds(col, HEAD)], preferred_element_type=jnp.float32)
            for i, p_ref in enumerate(piece_refs):
                acc = acc + jnp.dot(p1[:, i * width:(i + 1) * width], p_ref[1, :, pl.ds(col, HEAD)],
                                    preferred_element_type=jnp.float32)
            acc_ref[0, k] = acc
            m_ref[0, k] = jnp.broadcast_to(m, (nrow, HEAD))
            l_ref[0, k] = jnp.broadcast_to(l, (nrow, HEAD))
            return carry

        lax.fori_loop(0, kv_heads, head, 0)


def resp_kernel(meta_ref, q_ref, rk_hbm, acc_ref, m_ref, l_ref, out_ref, lse_ref, kv_buf, sems,
                *, rows, groups, kv_heads, scale, block, max_blocks):
    r = pl.program_id(0)
    c = meta_ref[meta_ref.shape[0] - 1]
    length = meta_ref[r]
    live_any = length > rows * c
    nrow = rows * groups
    kv_width = groups * HEAD
    limit = jnp.minimum(rows * c, length)
    nblocks = (limit + block - 1) // block

    @pl.when(jnp.logical_not(live_any))
    def _():
        out_ref[...] = jnp.zeros(out_ref.shape, out_ref.dtype)
        lse_ref[...] = jnp.zeros(lse_ref.shape, lse_ref.dtype)

    def run(n):
        width = n * block
        if n > 0:
            copies = [
                pltpu.make_async_copy(rk_hbm.at[h, r, pl.ds(0, width), :], kv_buf.at[h, pl.ds(0, width), :], sems.at[h])
                for h in range(2)
            ]
            for cp in copies:
                cp.start()
            for cp in copies:
                cp.wait()
        row_i = rows * c + lax.broadcasted_iota(jnp.int32, (nrow, 1), 0) % rows
        row_live = row_i < length

        def head(k, carry):
            col = pl.multiple_of(k * HEAD, HEAD)
            qoff = pl.multiple_of(k * kv_width, kv_width)
            m = m_ref[0, k]
            l = l_ref[0, k]
            acc = acc_ref[0, k]
            if n > 0:
                qk = stack_groups(q_ref[0, :, pl.ds(qoff, kv_width)], groups)
                s = scores(qk, kv_buf[0, 0:width, pl.ds(col, HEAD)], scale)
                live = lax.broadcasted_iota(jnp.int32, (nrow, width), 1) < limit
                s = jnp.where(live, s, NEG)
                m_new = jnp.maximum(m, jnp.max(s, axis=-1, keepdims=True))
                alpha = jnp.exp(m - m_new)
                m_wide = m_new if n == 1 else jnp.concatenate([m_new] * n, axis=1)
                p = jnp.where(live, jnp.exp(s - m_wide), 0.0)
                l = alpha * l + jnp.sum(p, axis=-1, keepdims=True)
                pv = jnp.dot(p.astype(jnp.bfloat16), kv_buf[1, 0:width, pl.ds(col, HEAD)],
                             preferred_element_type=jnp.float32)
                acc = alpha * acc + pv
                m = m_new
            o = jnp.where(row_live, acc / l, 0.0).astype(out_ref.dtype)
            for g in range(groups):
                out_ref[0, :, pl.ds(qoff + g * HEAD, HEAD)] = o[g * rows:(g + 1) * rows]
            lse = jnp.where(row_live, m + jnp.log(l), 0.0)
            lse_ref[0, k] = lse.T[0:1]
            return carry

        lax.fori_loop(0, kv_heads, head, 0)

    for n in range(max_blocks + 1):
        pl.when(live_any & (nblocks == n))(functools.partial(run, n))


def per_device(queries, prompt_kv, response_kv, lengths):
    resp_local, rows, width = queries.shape
    kv_width = prompt_kv.shape[2]
    kv_heads = kv_width // HEAD
    groups = width // kv_width
    nrow = rows * groups
    scale = 1.0 / math.sqrt(HEAD)
    c = lax.axis_index("ctx")
    meta = jnp.concatenate([lengths.astype(jnp.int32), c.astype(jnp.int32)[None]])

    ctx_prompt = lax.all_gather(prompt_kv, "ctx", axis=1, tiled=True)
    n_resp_dev = lax.axis_size("resp")
    pieces = [ctx_prompt] + [
        lax.ppermute(ctx_prompt, "resp", [(j, (j + shift) % n_resp_dev) for j in range(n_resp_dev)])
        for shift in range(1, n_resp_dev)
    ]
    full_resp = lax.all_gather(response_kv, "ctx", axis=2, tiled=True)
    n_piece = ctx_prompt.shape[1]
    n_prompt = n_piece * len(pieces)
    n_resp = full_resp.shape[2]

    q_spec = pl.BlockSpec((1, rows, width), lambda r, meta: (r, 0, 0))
    acc_spec = pl.BlockSpec((1, kv_heads, nrow, HEAD), lambda r, meta: (r, 0, 0, 0))

    params = pltpu.CompilerParams(vmem_limit_bytes=48 * 1024 * 1024)
    acc, m_rep, l_rep = pl.pallas_call(
        functools.partial(prompt_kernel, rows=rows, groups=groups, kv_heads=kv_heads, scale=scale, pieces=len(pieces)),
        grid_spec=pltpu.PrefetchScalarGridSpec(
            num_scalar_prefetch=1,
            grid=(resp_local,),
            in_specs=[
                q_spec,
                *[pl.BlockSpec((2, n_piece, kv_width), lambda r, meta: (0, 0, 0)) for _ in pieces],
                pl.BlockSpec((2, 1, rows, kv_width), lambda r, meta: (0, r, 0, 0)),
            ],
            out_specs=[acc_spec, acc_spec, acc_spec],
        ),
        out_shape=[
            jax.ShapeDtypeStruct((resp_local, kv_heads, nrow, HEAD), jnp.float32),
            jax.ShapeDtypeStruct((resp_local, kv_heads, nrow, HEAD), jnp.float32),
            jax.ShapeDtypeStruct((resp_local, kv_heads, nrow, HEAD), jnp.float32),
        ],
        compiler_params=params,
        cost_estimate=pl.CostEstimate(
            flops=4 * resp_local * kv_heads * nrow * (n_prompt + rows) * HEAD,
            transcendentals=resp_local * kv_heads * nrow * (n_prompt + rows),
            bytes_accessed=2 * (queries.size + n_prompt * prompt_kv.shape[0] * kv_width) + 4 * resp_local * kv_heads * nrow * HEAD,
        ),
    )(meta, queries, *pieces, response_kv)

    block = 128
    max_blocks = (n_resp - rows + block - 1) // block
    attended, lse_t = pl.pallas_call(
        functools.partial(resp_kernel, rows=rows, groups=groups, kv_heads=kv_heads, scale=scale, block=block,
                          max_blocks=max_blocks),
        grid_spec=pltpu.PrefetchScalarGridSpec(
            num_scalar_prefetch=1,
            grid=(resp_local,),
            in_specs=[
                q_spec,
                pl.BlockSpec(memory_space=pl.ANY),
                acc_spec,
                acc_spec,
                acc_spec,
            ],
            out_specs=[
                q_spec,
                pl.BlockSpec((1, kv_heads, 1, nrow), lambda r, meta: (r, 0, 0, 0)),
            ],
            scratch_shapes=[
                pltpu.VMEM((2, max_blocks * block, kv_width), jnp.bfloat16),
                pltpu.SemaphoreType.DMA((2,)),
            ],
        ),
        out_shape=[
            jax.ShapeDtypeStruct(queries.shape, queries.dtype),
            jax.ShapeDtypeStruct((resp_local, kv_heads, 1, nrow), jnp.float32),
        ],
        compiler_params=params,
        cost_estimate=pl.CostEstimate(
            flops=4 * resp_local * kv_heads * nrow * n_resp * HEAD // 2,
            transcendentals=resp_local * kv_heads * nrow * n_resp // 2,
            bytes_accessed=2 * (2 * queries.size + full_resp.size) + 4 * resp_local * kv_heads * nrow * HEAD,
        ),
    )(meta, queries, full_resp, acc, m_rep, l_rep)

    row_lse = (
        lse_t.reshape(resp_local, kv_heads, groups, rows)
        .transpose(0, 3, 1, 2)
        .reshape(resp_local, rows, kv_heads * groups)
    )
    return attended, row_lse


def solution(mesh):
    placed = (
        P("resp", "ctx", None),
        P(None, ("resp", "ctx"), None),
        P(None, "resp", "ctx", None),
        P("resp"),
    )
    return jax.shard_map(
        per_device,
        mesh=mesh,
        in_specs=placed,
        out_specs=(P("resp", "ctx", None), P("resp", "ctx", None)),
        check_vma=False,
    )
```

```python
import functools
import math

import jax
import jax.numpy as jnp
from jax import lax
from jax.experimental import pallas as pl
from jax.experimental.pallas import tpu as pltpu
from jax.sharding import PartitionSpec as P

HEAD = 128
NEG = -1e30
LN2 = math.log(2.0)


def stack_groups(q, groups):
    return jnp.concatenate([q[:, g * HEAD:(g + 1) * HEAD] for g in range(groups)], axis=0)


def scores(qk, keys, scale):
    return lax.dot_general(qk, keys, (((1,), (1,)), ((), ())), preferred_element_type=jnp.float32) * scale


def prompt_kernel(meta_ref, q_ref, *refs, rows, groups, kv_heads, scale, pieces):
    piece_refs = refs[:pieces]
    own_ref, acc_ref, m_ref, l_ref = refs[pieces:]
    r = pl.program_id(0)
    c = meta_ref[meta_ref.shape[0] - 1]
    length = meta_ref[r]
    nrow = rows * groups
    kv_width = groups * HEAD

    @pl.when(length > rows * c)
    def _():
        row_i = rows * c + lax.broadcasted_iota(jnp.int32, (nrow, 1), 0) % rows
        j = rows * c + lax.broadcasted_iota(jnp.int32, (nrow, rows), 1)
        live = (j <= row_i) & (j < length)
        n_prompt = sum(p_ref.shape[1] for p_ref in piece_refs)
        ones_prompt = jnp.ones((n_prompt, HEAD), jnp.bfloat16)
        ones_own = jnp.ones((rows, HEAD), jnp.bfloat16)

        def head(k, carry):
            col = pl.multiple_of(k * HEAD, HEAD)
            qk = stack_groups(q_ref[0, :, pl.ds(pl.multiple_of(k * kv_width, kv_width), kv_width)], groups)
            keys = jnp.concatenate([p_ref[0, :, pl.ds(col, HEAD)] for p_ref in piece_refs], axis=0)
            vals = jnp.concatenate([p_ref[1, :, pl.ds(col, HEAD)] for p_ref in piece_refs], axis=0)
            s1 = scores(qk, keys, scale)
            s2 = jnp.where(live, scores(qk, own_ref[0, 0, :, pl.ds(col, HEAD)], scale), NEG)
            m = jnp.maximum(jnp.max(s1, axis=-1, keepdims=True), jnp.max(s2, axis=-1, keepdims=True))
            p1 = jnp.exp2(s1 - m).astype(jnp.bfloat16)
            p2 = jnp.where(live, jnp.exp2(s2 - m), 0.0).astype(jnp.bfloat16)
            own_vals = own_ref[1, 0, :, pl.ds(col, HEAD)]
            acc = jnp.dot(p1, vals, preferred_element_type=jnp.float32)
            acc = acc + jnp.dot(p2, own_vals, preferred_element_type=jnp.float32)
            l = jnp.dot(p1, ones_prompt, preferred_element_type=jnp.float32)
            l = l + jnp.dot(p2, ones_own, preferred_element_type=jnp.float32)
            acc_ref[0, k] = acc
            m_ref[0, k] = jnp.broadcast_to(m, (nrow, HEAD))
            l_ref[0, k] = l
            return carry

        lax.fori_loop(0, kv_heads, head, 0)


def resp_kernel(meta_ref, q_ref, rk_hbm, acc_ref, m_ref, l_ref, out_ref, lse_ref, kv_buf, sems,
                *, rows, groups, kv_heads, scale, block, max_blocks):
    r = pl.program_id(0)
    c = meta_ref[meta_ref.shape[0] - 1]
    length = meta_ref[r]
    live_any = length > rows * c
    nrow = rows * groups
    kv_width = groups * HEAD
    limit = jnp.minimum(rows * c, length)
    nblocks = (limit + block - 1) // block

    @pl.when(jnp.logical_not(live_any))
    def _():
        out_ref[...] = jnp.zeros(out_ref.shape, out_ref.dtype)
        lse_ref[...] = jnp.zeros(lse_ref.shape, lse_ref.dtype)

    def run(n):
        width = n * block
        if n > 0:
            copies = [
                pltpu.make_async_copy(rk_hbm.at[h, r, pl.ds(0, width), :], kv_buf.at[h, pl.ds(0, width), :], sems.at[h])
                for h in range(2)
            ]
            for cp in copies:
                cp.start()
            for cp in copies:
                cp.wait()
        row_i = rows * c + lax.broadcasted_iota(jnp.int32, (nrow, 1), 0) % rows
        row_live = row_i < length
        ones = jnp.ones((max(width, 8), HEAD), jnp.bfloat16)

        def head(k, carry):
            col = pl.multiple_of(k * HEAD, HEAD)
            qoff = pl.multiple_of(k * kv_width, kv_width)
            m = m_ref[0, k]
            l = l_ref[0, k]
            acc = acc_ref[0, k]
            if n > 0:
                qk = stack_groups(q_ref[0, :, pl.ds(qoff, kv_width)], groups)
                s = scores(qk, kv_buf[0, 0:width, pl.ds(col, HEAD)], scale)
                live = lax.broadcasted_iota(jnp.int32, (nrow, width), 1) < limit
                s = jnp.where(live, s, NEG)
                m_new = jnp.maximum(m, jnp.max(s, axis=-1, keepdims=True))
                alpha = jnp.exp2(m - m_new)
                m_wide = m_new if n == 1 else jnp.concatenate([m_new] * n, axis=1)
                p = jnp.where(live, jnp.exp2(s - m_wide), 0.0).astype(jnp.bfloat16)
                l = alpha * l + jnp.dot(p, ones, preferred_element_type=jnp.float32)
                pv = jnp.dot(p, kv_buf[1, 0:width, pl.ds(col, HEAD)], preferred_element_type=jnp.float32)
                acc = alpha * acc + pv
                m = m_new
            o = jnp.where(row_live, acc / l, 0.0).astype(out_ref.dtype)
            for g in range(groups):
                out_ref[0, :, pl.ds(qoff + g * HEAD, HEAD)] = o[g * rows:(g + 1) * rows]
            lse = jnp.where(row_live, m * LN2 + jnp.log(l), 0.0)
            lse_ref[0, k] = lse.T[0:1]
            return carry

        lax.fori_loop(0, kv_heads, head, 0)

    for n in range(max_blocks + 1):
        pl.when(live_any & (nblocks == n))(functools.partial(run, n))


def per_device(queries, prompt_kv, response_kv, lengths):
    resp_local, rows, width = queries.shape
    kv_width = prompt_kv.shape[2]
    kv_heads = kv_width // HEAD
    groups = width // kv_width
    nrow = rows * groups
    scale = math.log2(math.e) / math.sqrt(HEAD)
    c = lax.axis_index("ctx")
    meta = jnp.concatenate([lengths.astype(jnp.int32), c.astype(jnp.int32)[None]])

    ctx_prompt = lax.all_gather(prompt_kv, "ctx", axis=1, tiled=True)
    n_resp_dev = lax.axis_size("resp")
    pieces = [ctx_prompt] + [
        lax.ppermute(ctx_prompt, "resp", [(j, (j + shift) % n_resp_dev) for j in range(n_resp_dev)])
        for shift in range(1, n_resp_dev)
    ]
    full_resp = lax.all_gather(response_kv, "ctx", axis=2, tiled=True)
    n_piece = ctx_prompt.shape[1]
    n_prompt = n_piece * len(pieces)
    n_resp = full_resp.shape[2]

    q_spec = pl.BlockSpec((1, rows, width), lambda r, meta: (r, 0, 0))
    acc_spec = pl.BlockSpec((1, kv_heads, nrow, HEAD), lambda r, meta: (r, 0, 0, 0))

    params = pltpu.CompilerParams(vmem_limit_bytes=48 * 1024 * 1024)
    acc, m_rep, l_rep = pl.pallas_call(
        functools.partial(prompt_kernel, rows=rows, groups=groups, kv_heads=kv_heads, scale=scale, pieces=len(pieces)),
        grid_spec=pltpu.PrefetchScalarGridSpec(
            num_scalar_prefetch=1,
            grid=(resp_local,),
            in_specs=[
                q_spec,
                *[pl.BlockSpec((2, n_piece, kv_width), lambda r, meta: (0, 0, 0)) for _ in pieces],
                pl.BlockSpec((2, 1, rows, kv_width), lambda r, meta: (0, r, 0, 0)),
            ],
            out_specs=[acc_spec, acc_spec, acc_spec],
        ),
        out_shape=[
            jax.ShapeDtypeStruct((resp_local, kv_heads, nrow, HEAD), jnp.float32),
            jax.ShapeDtypeStruct((resp_local, kv_heads, nrow, HEAD), jnp.float32),
            jax.ShapeDtypeStruct((resp_local, kv_heads, nrow, HEAD), jnp.float32),
        ],
        compiler_params=params,
        cost_estimate=pl.CostEstimate(
            flops=4 * resp_local * kv_heads * nrow * (n_prompt + rows) * HEAD,
            transcendentals=resp_local * kv_heads * nrow * (n_prompt + rows),
            bytes_accessed=2 * (queries.size + n_prompt * prompt_kv.shape[0] * kv_width) + 4 * resp_local * kv_heads * nrow * HEAD,
        ),
    )(meta, queries, *pieces, response_kv)

    block = 128
    max_blocks = (n_resp - rows + block - 1) // block
    attended, lse_t = pl.pallas_call(
        functools.partial(resp_kernel, rows=rows, groups=groups, kv_heads=kv_heads, scale=scale, block=block,
                          max_blocks=max_blocks),
        grid_spec=pltpu.PrefetchScalarGridSpec(
            num_scalar_prefetch=1,
            grid=(resp_local,),
            in_specs=[
                q_spec,
                pl.BlockSpec(memory_space=pl.ANY),
                acc_spec,
                acc_spec,
                acc_spec,
            ],
            out_specs=[
                q_spec,
                pl.BlockSpec((1, kv_heads, 1, nrow), lambda r, meta: (r, 0, 0, 0)),
            ],
            scratch_shapes=[
                pltpu.VMEM((2, max_blocks * block, kv_width), jnp.bfloat16),
                pltpu.SemaphoreType.DMA((2,)),
            ],
        ),
        out_shape=[
            jax.ShapeDtypeStruct(queries.shape, queries.dtype),
            jax.ShapeDtypeStruct((resp_local, kv_heads, 1, nrow), jnp.float32),
        ],
        compiler_params=params,
        cost_estimate=pl.CostEstimate(
            flops=4 * resp_local * kv_heads * nrow * n_resp * HEAD // 2,
            transcendentals=resp_local * kv_heads * nrow * n_resp // 2,
            bytes_accessed=2 * (2 * queries.size + full_resp.size) + 4 * resp_local * kv_heads * nrow * HEAD,
        ),
    )(meta, queries, full_resp, acc, m_rep, l_rep)

    row_lse = (
        lse_t.reshape(resp_local, kv_heads, groups, rows)
        .transpose(0, 3, 1, 2)
        .reshape(resp_local, rows, kv_heads * groups)
    )
    return attended, row_lse


def solution(mesh):
    placed = (
        P("resp", "ctx", None),
        P(None, ("resp", "ctx"), None),
        P(None, "resp", "ctx", None),
        P("resp"),
    )
    return jax.shard_map(
        per_device,
        mesh=mesh,
        in_specs=placed,
        out_specs=(P("resp", "ctx", None), P("resp", "ctx", None)),
        check_vma=False,
    )
```

```python
import functools
import math

import jax
import jax.numpy as jnp
from jax import lax
from jax.experimental import pallas as pl
from jax.experimental.pallas import tpu as pltpu
from jax.sharding import PartitionSpec as P

HEAD = 128
NEG = -1e30
LN2 = math.log(2.0)


def stack_groups(q, groups):
    return jnp.concatenate([q[:, g * HEAD:(g + 1) * HEAD] for g in range(groups)], axis=0)


def scores(qk, keys, scale):
    return lax.dot_general(qk, keys, (((1,), (1,)), ((), ())), preferred_element_type=jnp.float32) * scale


def prompt_kernel(meta_ref, q_ref, *refs, rows, groups, kv_heads, scale, pieces):
    piece_refs = refs[:pieces]
    own_ref, acc_ref, m_ref, l_ref = refs[pieces:]
    r = pl.program_id(0)
    c = meta_ref[meta_ref.shape[0] - 1]
    length = meta_ref[r]
    nrow = rows * groups
    kv_width = groups * HEAD

    @pl.when(length > rows * c)
    def _():
        row_i = rows * c + lax.broadcasted_iota(jnp.int32, (nrow, 1), 0) % rows
        j = rows * c + lax.broadcasted_iota(jnp.int32, (nrow, rows), 1)
        live = (j <= row_i) & (j < length)
        n_prompt = sum(p_ref.shape[1] for p_ref in piece_refs)
        ones_prompt = jnp.ones((n_prompt, HEAD), jnp.bfloat16)
        ones_own = jnp.ones((rows, HEAD), jnp.bfloat16)

        def head(k, carry):
            col = pl.multiple_of(k * HEAD, HEAD)
            qk = stack_groups(q_ref[0, :, pl.ds(pl.multiple_of(k * kv_width, kv_width), kv_width)], groups)
            keys = jnp.concatenate([p_ref[0, :, pl.ds(col, HEAD)] for p_ref in piece_refs], axis=0)
            vals = jnp.concatenate([p_ref[1, :, pl.ds(col, HEAD)] for p_ref in piece_refs], axis=0)
            s1 = scores(qk, keys, scale)
            s2 = jnp.where(live, scores(qk, own_ref[0, 0, :, pl.ds(col, HEAD)], scale), NEG)
            m = jnp.maximum(jnp.max(s1, axis=-1, keepdims=True), jnp.max(s2, axis=-1, keepdims=True))
            p1 = jnp.exp2(s1 - m).astype(jnp.bfloat16)
            p2 = jnp.where(live, jnp.exp2(s2 - m), 0.0).astype(jnp.bfloat16)
            own_vals = own_ref[1, 0, :, pl.ds(col, HEAD)]
            acc = jnp.dot(p1, vals, preferred_element_type=jnp.float32)
            acc = acc + jnp.dot(p2, own_vals, preferred_element_type=jnp.float32)
            l = jnp.dot(p1, ones_prompt, preferred_element_type=jnp.float32)
            l = l + jnp.dot(p2, ones_own, preferred_element_type=jnp.float32)
            acc_ref[0, k] = acc
            m_ref[0, k] = jnp.broadcast_to(m, (nrow, HEAD))
            l_ref[0, k] = l
            return carry

        lax.fori_loop(0, kv_heads, head, 0)


def resp_kernel(meta_ref, q_ref, rk_hbm, acc_ref, m_ref, l_ref, out_ref, lse_ref, kv_buf, sems,
                *, rows, groups, kv_heads, scale, block, max_blocks):
    r = pl.program_id(0)
    c = meta_ref[meta_ref.shape[0] - 1]
    length = meta_ref[r]
    live_any = length > rows * c
    nrow = rows * groups
    kv_width = groups * HEAD
    limit = jnp.minimum(rows * c, length)
    nblocks = (limit + block - 1) // block

    @pl.when(jnp.logical_not(live_any))
    def _():
        out_ref[...] = jnp.zeros(out_ref.shape, out_ref.dtype)
        lse_ref[...] = jnp.zeros(lse_ref.shape, lse_ref.dtype)

    def run(n):
        width = n * block
        if n > 0:
            chunk = rk_hbm.shape[3]
            copies = [
                pltpu.make_async_copy(rk_hbm.at[i, h, r], kv_buf.at[h, pl.ds(i * chunk, chunk), :], sems.at[h, i])
                for h in range(2)
                for i in range(width // chunk)
            ]
            for cp in copies:
                cp.start()
            for cp in copies:
                cp.wait()
        row_i = rows * c + lax.broadcasted_iota(jnp.int32, (nrow, 1), 0) % rows
        row_live = row_i < length
        ones = jnp.ones((max(width, 8), HEAD), jnp.bfloat16)

        def head(k, carry):
            col = pl.multiple_of(k * HEAD, HEAD)
            qoff = pl.multiple_of(k * kv_width, kv_width)
            m = m_ref[0, k]
            l = l_ref[0, k]
            acc = acc_ref[0, k]
            if n > 0:
                qk = stack_groups(q_ref[0, :, pl.ds(qoff, kv_width)], groups)
                s = scores(qk, kv_buf[0, 0:width, pl.ds(col, HEAD)], scale)
                live = lax.broadcasted_iota(jnp.int32, (nrow, width), 1) < limit
                s = jnp.where(live, s, NEG)
                m_new = jnp.maximum(m, jnp.max(s, axis=-1, keepdims=True))
                alpha = jnp.exp2(m - m_new)
                m_wide = m_new if n == 1 else jnp.concatenate([m_new] * n, axis=1)
                p = jnp.where(live, jnp.exp2(s - m_wide), 0.0).astype(jnp.bfloat16)
                l = alpha * l + jnp.dot(p, ones, preferred_element_type=jnp.float32)
                pv = jnp.dot(p, kv_buf[1, 0:width, pl.ds(col, HEAD)], preferred_element_type=jnp.float32)
                acc = alpha * acc + pv
                m = m_new
            o = jnp.where(row_live, acc / l, 0.0).astype(out_ref.dtype)
            for g in range(groups):
                out_ref[0, :, pl.ds(qoff + g * HEAD, HEAD)] = o[g * rows:(g + 1) * rows]
            lse = jnp.where(row_live, m * LN2 + jnp.log(l), 0.0)
            lse_ref[0, k] = lse.T[0:1]
            return carry

        lax.fori_loop(0, kv_heads, head, 0)

    for n in range(max_blocks + 1):
        pl.when(live_any & (nblocks == n))(functools.partial(run, n))


def per_device(queries, prompt_kv, response_kv, lengths):
    resp_local, rows, width = queries.shape
    kv_width = prompt_kv.shape[2]
    kv_heads = kv_width // HEAD
    groups = width // kv_width
    nrow = rows * groups
    scale = math.log2(math.e) / math.sqrt(HEAD)
    c = lax.axis_index("ctx")
    meta = jnp.concatenate([lengths.astype(jnp.int32), c.astype(jnp.int32)[None]])

    ctx_prompt = lax.all_gather(prompt_kv, "ctx", axis=1, tiled=True)
    n_resp_dev = lax.axis_size("resp")
    pieces = [ctx_prompt] + [
        lax.ppermute(ctx_prompt, "resp", [(j, (j + shift) % n_resp_dev) for j in range(n_resp_dev)])
        for shift in range(1, n_resp_dev)
    ]
    full_resp = lax.all_gather(response_kv, "ctx", axis=0, tiled=False)
    n_piece = ctx_prompt.shape[1]
    n_prompt = n_piece * len(pieces)
    n_resp = full_resp.shape[0] * full_resp.shape[3]

    q_spec = pl.BlockSpec((1, rows, width), lambda r, meta: (r, 0, 0))
    acc_spec = pl.BlockSpec((1, kv_heads, nrow, HEAD), lambda r, meta: (r, 0, 0, 0))

    params = pltpu.CompilerParams(vmem_limit_bytes=48 * 1024 * 1024)
    acc, m_rep, l_rep = pl.pallas_call(
        functools.partial(prompt_kernel, rows=rows, groups=groups, kv_heads=kv_heads, scale=scale, pieces=len(pieces)),
        grid_spec=pltpu.PrefetchScalarGridSpec(
            num_scalar_prefetch=1,
            grid=(resp_local,),
            in_specs=[
                q_spec,
                *[pl.BlockSpec((2, n_piece, kv_width), lambda r, meta: (0, 0, 0)) for _ in pieces],
                pl.BlockSpec((2, 1, rows, kv_width), lambda r, meta: (0, r, 0, 0)),
            ],
            out_specs=[acc_spec, acc_spec, acc_spec],
        ),
        out_shape=[
            jax.ShapeDtypeStruct((resp_local, kv_heads, nrow, HEAD), jnp.float32),
            jax.ShapeDtypeStruct((resp_local, kv_heads, nrow, HEAD), jnp.float32),
            jax.ShapeDtypeStruct((resp_local, kv_heads, nrow, HEAD), jnp.float32),
        ],
        compiler_params=params,
        cost_estimate=pl.CostEstimate(
            flops=4 * resp_local * kv_heads * nrow * (n_prompt + rows) * HEAD,
            transcendentals=resp_local * kv_heads * nrow * (n_prompt + rows),
            bytes_accessed=2 * (queries.size + n_prompt * prompt_kv.shape[0] * kv_width) + 4 * resp_local * kv_heads * nrow * HEAD,
        ),
    )(meta, queries, *pieces, response_kv)

    block = 128
    max_blocks = (n_resp - rows + block - 1) // block
    attended, lse_t = pl.pallas_call(
        functools.partial(resp_kernel, rows=rows, groups=groups, kv_heads=kv_heads, scale=scale, block=block,
                          max_blocks=max_blocks),
        grid_spec=pltpu.PrefetchScalarGridSpec(
            num_scalar_prefetch=1,
            grid=(resp_local,),
            in_specs=[
                q_spec,
                pl.BlockSpec(memory_space=pl.ANY),
                acc_spec,
                acc_spec,
                acc_spec,
            ],
            out_specs=[
                q_spec,
                pl.BlockSpec((1, kv_heads, 1, nrow), lambda r, meta: (r, 0, 0, 0)),
            ],
            scratch_shapes=[
                pltpu.VMEM((2, max_blocks * block, kv_width), jnp.bfloat16),
                pltpu.SemaphoreType.DMA((2, full_resp.shape[0])),
            ],
        ),
        out_shape=[
            jax.ShapeDtypeStruct(queries.shape, queries.dtype),
            jax.ShapeDtypeStruct((resp_local, kv_heads, 1, nrow), jnp.float32),
        ],
        compiler_params=params,
        cost_estimate=pl.CostEstimate(
            flops=4 * resp_local * kv_heads * nrow * n_resp * HEAD // 2,
            transcendentals=resp_local * kv_heads * nrow * n_resp // 2,
            bytes_accessed=2 * (2 * queries.size + full_resp.size) + 4 * resp_local * kv_heads * nrow * HEAD,
        ),
    )(meta, queries, full_resp, acc, m_rep, l_rep)

    row_lse = (
        lse_t.reshape(resp_local, kv_heads, groups, rows)
        .transpose(0, 3, 1, 2)
        .reshape(resp_local, rows, kv_heads * groups)
    )
    return attended, row_lse


def solution(mesh):
    placed = (
        P("resp", "ctx", None),
        P(None, ("resp", "ctx"), None),
        P(None, "resp", "ctx", None),
        P("resp"),
    )
    return jax.shard_map(
        per_device,
        mesh=mesh,
        in_specs=placed,
        out_specs=(P("resp", "ctx", None), P("resp", "ctx", None)),
        check_vma=False,
    )
```

```python
import functools
import math

import jax
import jax.numpy as jnp
from jax import lax
from jax.experimental import pallas as pl
from jax.experimental.pallas import tpu as pltpu
from jax.sharding import PartitionSpec as P

HEAD = 128
NEG = -1e30
LN2 = math.log(2.0)


def stack_groups(q, groups):
    return jnp.concatenate([q[:, g * HEAD:(g + 1) * HEAD] for g in range(groups)], axis=0)


def scores(qk, keys, scale):
    return lax.dot_general(qk, keys, (((1,), (1,)), ((), ())), preferred_element_type=jnp.float32) * scale


def prompt_kernel(meta_ref, q_ref, *refs, rows, groups, kv_heads, scale, pieces, own, carry_in):
    piece_refs = refs[:pieces]
    rest = list(refs[pieces:])
    own_ref = rest.pop(0) if own else None
    in_refs = [rest.pop(0) for _ in range(3)] if carry_in else None
    acc_ref, m_ref, l_ref = rest
    r = pl.program_id(0)
    c = meta_ref[meta_ref.shape[0] - 1]
    length = meta_ref[r]
    nrow = rows * groups
    kv_width = groups * HEAD

    @pl.when(length > rows * c)
    def _():
        row_i = rows * c + lax.broadcasted_iota(jnp.int32, (nrow, 1), 0) % rows
        j = rows * c + lax.broadcasted_iota(jnp.int32, (nrow, rows), 1)
        live = (j <= row_i) & (j < length)
        n_prompt = sum(p_ref.shape[1] for p_ref in piece_refs)
        ones_prompt = jnp.ones((n_prompt, HEAD), jnp.bfloat16)
        ones_own = jnp.ones((rows, HEAD), jnp.bfloat16)

        def head(k, carry):
            col = pl.multiple_of(k * HEAD, HEAD)
            qk = stack_groups(q_ref[0, :, pl.ds(pl.multiple_of(k * kv_width, kv_width), kv_width)], groups)
            keys = jnp.concatenate([p_ref[0, :, pl.ds(col, HEAD)] for p_ref in piece_refs], axis=0)
            vals = jnp.concatenate([p_ref[1, :, pl.ds(col, HEAD)] for p_ref in piece_refs], axis=0)
            s1 = scores(qk, keys, scale)
            m = jnp.max(s1, axis=-1, keepdims=True)
            if own:
                s2 = jnp.where(live, scores(qk, own_ref[0, 0, :, pl.ds(col, HEAD)], scale), NEG)
                m = jnp.maximum(m, jnp.max(s2, axis=-1, keepdims=True))
            if carry_in:
                m_in = in_refs[1][0, k]
                m = jnp.maximum(m_in[:, 0:1], m)
                alpha = jnp.exp2(m_in - m)
            m_rep = jnp.broadcast_to(m, (nrow, HEAD))
            p1 = jnp.exp2(s1 - m).astype(jnp.bfloat16)
            acc = jnp.dot(p1, vals, preferred_element_type=jnp.float32)
            l = jnp.dot(p1, ones_prompt, preferred_element_type=jnp.float32)
            if own:
                p2 = jnp.where(live, jnp.exp2(s2 - m), 0.0).astype(jnp.bfloat16)
                acc = acc + jnp.dot(p2, own_ref[1, 0, :, pl.ds(col, HEAD)], preferred_element_type=jnp.float32)
                l = l + jnp.dot(p2, ones_own, preferred_element_type=jnp.float32)
            if carry_in:
                acc = alpha * in_refs[0][0, k] + acc
                l = alpha * in_refs[2][0, k] + l
            acc_ref[0, k] = acc
            m_ref[0, k] = m_rep
            l_ref[0, k] = l
            return carry

        lax.fori_loop(0, kv_heads, head, 0)


def resp_kernel(meta_ref, q_ref, rk_hbm, acc_ref, m_ref, l_ref, out_ref, lse_ref, kv_buf, sems,
                *, rows, groups, kv_heads, scale, block, max_blocks):
    r = pl.program_id(0)
    c = meta_ref[meta_ref.shape[0] - 1]
    length = meta_ref[r]
    live_any = length > rows * c
    nrow = rows * groups
    kv_width = groups * HEAD
    limit = jnp.minimum(rows * c, length)
    nblocks = (limit + block - 1) // block

    @pl.when(jnp.logical_not(live_any))
    def _():
        out_ref[...] = jnp.zeros(out_ref.shape, out_ref.dtype)
        lse_ref[...] = jnp.zeros(lse_ref.shape, lse_ref.dtype)

    def run(n):
        width = n * block
        if n > 0:
            chunk = rk_hbm.shape[3]
            copies = [
                pltpu.make_async_copy(rk_hbm.at[i, h, r], kv_buf.at[h, pl.ds(i * chunk, chunk), :], sems.at[h, i])
                for h in range(2)
                for i in range(width // chunk)
            ]
            for cp in copies:
                cp.start()
            for cp in copies:
                cp.wait()
        row_i = rows * c + lax.broadcasted_iota(jnp.int32, (nrow, 1), 0) % rows
        row_live = row_i < length
        ones = jnp.ones((max(width, 8), HEAD), jnp.bfloat16)

        def head(k, carry):
            col = pl.multiple_of(k * HEAD, HEAD)
            qoff = pl.multiple_of(k * kv_width, kv_width)
            m = m_ref[0, k]
            l = l_ref[0, k]
            acc = acc_ref[0, k]
            if n > 0:
                qk = stack_groups(q_ref[0, :, pl.ds(qoff, kv_width)], groups)
                s = scores(qk, kv_buf[0, 0:width, pl.ds(col, HEAD)], scale)
                live = lax.broadcasted_iota(jnp.int32, (nrow, width), 1) < limit
                s = jnp.where(live, s, NEG)
                m_new = jnp.maximum(m, jnp.max(s, axis=-1, keepdims=True))
                alpha = jnp.exp2(m - m_new)
                m_wide = m_new if n == 1 else jnp.concatenate([m_new] * n, axis=1)
                p = jnp.where(live, jnp.exp2(s - m_wide), 0.0).astype(jnp.bfloat16)
                l = alpha * l + jnp.dot(p, ones, preferred_element_type=jnp.float32)
                pv = jnp.dot(p, kv_buf[1, 0:width, pl.ds(col, HEAD)], preferred_element_type=jnp.float32)
                acc = alpha * acc + pv
                m = m_new
            o = jnp.where(row_live, acc / l, 0.0).astype(out_ref.dtype)
            for g in range(groups):
                out_ref[0, :, pl.ds(qoff + g * HEAD, HEAD)] = o[g * rows:(g + 1) * rows]
            lse = jnp.where(row_live, m * LN2 + jnp.log(l), 0.0)
            lse_ref[0, k] = lse.T[0:1]
            return carry

        lax.fori_loop(0, kv_heads, head, 0)

    for n in range(max_blocks + 1):
        pl.when(live_any & (nblocks == n))(functools.partial(run, n))


def per_device(queries, prompt_kv, response_kv, lengths):
    resp_local, rows, width = queries.shape
    kv_width = prompt_kv.shape[2]
    kv_heads = kv_width // HEAD
    groups = width // kv_width
    nrow = rows * groups
    scale = math.log2(math.e) / math.sqrt(HEAD)
    c = lax.axis_index("ctx")
    meta = jnp.concatenate([lengths.astype(jnp.int32), c.astype(jnp.int32)[None]])

    ctx_prompt = lax.all_gather(prompt_kv, "ctx", axis=1, tiled=True)
    n_resp_dev = lax.axis_size("resp")
    pieces = [ctx_prompt] + [
        lax.ppermute(ctx_prompt, "resp", [(j, (j + shift) % n_resp_dev) for j in range(n_resp_dev)])
        for shift in range(1, n_resp_dev)
    ]
    full_resp = lax.all_gather(response_kv, "ctx", axis=0, tiled=False)
    n_piece = ctx_prompt.shape[1]
    n_prompt = n_piece * len(pieces)
    n_resp = full_resp.shape[0] * full_resp.shape[3]

    q_spec = pl.BlockSpec((1, rows, width), lambda r, meta: (r, 0, 0))
    acc_spec = pl.BlockSpec((1, kv_heads, nrow, HEAD), lambda r, meta: (r, 0, 0, 0))

    params = pltpu.CompilerParams(vmem_limit_bytes=48 * 1024 * 1024)
    state_shape = [jax.ShapeDtypeStruct((resp_local, kv_heads, nrow, HEAD), jnp.float32)] * 3

    def prompt_pass(chunks, own, carry_in, state):
        keys_here = n_piece * len(chunks) + (rows if own else 0)
        return pl.pallas_call(
            functools.partial(prompt_kernel, rows=rows, groups=groups, kv_heads=kv_heads, scale=scale,
                              pieces=len(chunks), own=own, carry_in=carry_in),
            grid_spec=pltpu.PrefetchScalarGridSpec(
                num_scalar_prefetch=1,
                grid=(resp_local,),
                in_specs=[
                    q_spec,
                    *[pl.BlockSpec((2, n_piece, kv_width), lambda r, meta: (0, 0, 0)) for _ in chunks],
                    *([pl.BlockSpec((2, 1, rows, kv_width), lambda r, meta: (0, r, 0, 0))] if own else []),
                    *([acc_spec] * 3 if carry_in else []),
                ],
                out_specs=[acc_spec, acc_spec, acc_spec],
            ),
            out_shape=state_shape,
            compiler_params=params,
            cost_estimate=pl.CostEstimate(
                flops=6 * resp_local * kv_heads * nrow * keys_here * HEAD,
                transcendentals=resp_local * kv_heads * nrow * keys_here,
                bytes_accessed=2 * (queries.size + keys_here * 2 * kv_width) + 12 * resp_local * kv_heads * nrow * HEAD,
            ),
        )(meta, queries, *chunks, *([response_kv] if own else []), *state)

    first = prompt_pass(pieces[:1], True, False, [])
    acc, m_rep, l_rep = prompt_pass(pieces[1:], False, True, list(first))

    block = 128
    max_blocks = (n_resp - rows + block - 1) // block
    attended, lse_t = pl.pallas_call(
        functools.partial(resp_kernel, rows=rows, groups=groups, kv_heads=kv_heads, scale=scale, block=block,
                          max_blocks=max_blocks),
        grid_spec=pltpu.PrefetchScalarGridSpec(
            num_scalar_prefetch=1,
            grid=(resp_local,),
            in_specs=[
                q_spec,
                pl.BlockSpec(memory_space=pl.ANY),
                acc_spec,
                acc_spec,
                acc_spec,
            ],
            out_specs=[
                q_spec,
                pl.BlockSpec((1, kv_heads, 1, nrow), lambda r, meta: (r, 0, 0, 0)),
            ],
            scratch_shapes=[
                pltpu.VMEM((2, max_blocks * block, kv_width), jnp.bfloat16),
                pltpu.SemaphoreType.DMA((2, full_resp.shape[0])),
            ],
        ),
        out_shape=[
            jax.ShapeDtypeStruct(queries.shape, queries.dtype),
            jax.ShapeDtypeStruct((resp_local, kv_heads, 1, nrow), jnp.float32),
        ],
        compiler_params=params,
        cost_estimate=pl.CostEstimate(
            flops=4 * resp_local * kv_heads * nrow * n_resp * HEAD // 2,
            transcendentals=resp_local * kv_heads * nrow * n_resp // 2,
            bytes_accessed=2 * (2 * queries.size + full_resp.size) + 4 * resp_local * kv_heads * nrow * HEAD,
        ),
    )(meta, queries, full_resp, acc, m_rep, l_rep)

    row_lse = (
        lse_t.reshape(resp_local, kv_heads, groups, rows)
        .transpose(0, 3, 1, 2)
        .reshape(resp_local, rows, kv_heads * groups)
    )
    return attended, row_lse


def solution(mesh):
    placed = (
        P("resp", "ctx", None),
        P(None, ("resp", "ctx"), None),
        P(None, "resp", "ctx", None),
        P("resp"),
    )
    return jax.shard_map(
        per_device,
        mesh=mesh,
        in_specs=placed,
        out_specs=(P("resp", "ctx", None), P("resp", "ctx", None)),
        check_vma=False,
    )
```

```python
import functools
import math

import jax
import jax.numpy as jnp
from jax import lax
from jax.experimental import pallas as pl
from jax.experimental.pallas import tpu as pltpu
from jax.sharding import PartitionSpec as P

HEAD = 128
NEG = -1e30
LN2 = math.log(2.0)
HALF = 64


def stack_groups(q, groups):
    return jnp.concatenate([q[:, g * HEAD:(g + 1) * HEAD] for g in range(groups)], axis=0)


def scores(qk, keys, scale):
    return lax.dot_general(qk, keys, (((1,), (1,)), ((), ())), preferred_element_type=jnp.float32) * scale


def prompt_kernel(meta_ref, q_ref, *refs, rows, groups, kv_heads, scale, pieces, own, carry_in):
    piece_refs = refs[:pieces]
    rest = list(refs[pieces:])
    own_ref = rest.pop(0) if own else None
    in_refs = [rest.pop(0) for _ in range(2)] if carry_in else None
    acc_ref, ml_ref = rest
    r = pl.program_id(0)
    c = meta_ref[meta_ref.shape[0] - 1]
    length = meta_ref[r]
    nrow = rows * groups
    kv_width = groups * HEAD

    @pl.when(length > rows * c)
    def _():
        row_i = rows * c + lax.broadcasted_iota(jnp.int32, (nrow, 1), 0) % rows
        j = rows * c + lax.broadcasted_iota(jnp.int32, (nrow, rows), 1)
        live = (j <= row_i) & (j < length)
        n_prompt = sum(p_ref.shape[1] for p_ref in piece_refs)
        ones_prompt = jnp.ones((n_prompt, HEAD), jnp.bfloat16)
        ones_own = jnp.ones((rows, HEAD), jnp.bfloat16)

        def head(k, carry):
            col = pl.multiple_of(k * HEAD, HEAD)
            qk = stack_groups(q_ref[0, :, pl.ds(pl.multiple_of(k * kv_width, kv_width), kv_width)], groups)
            keys = jnp.concatenate([p_ref[0, :, pl.ds(col, HEAD)] for p_ref in piece_refs], axis=0)
            vals = jnp.concatenate([p_ref[1, :, pl.ds(col, HEAD)] for p_ref in piece_refs], axis=0)
            s1 = scores(qk, keys, scale)
            m = jnp.max(s1, axis=-1, keepdims=True)
            if own:
                s2 = jnp.where(live, scores(qk, own_ref[0, 0, :, pl.ds(col, HEAD)], scale), NEG)
                m = jnp.maximum(m, jnp.max(s2, axis=-1, keepdims=True))
            if carry_in:
                ml_in = in_refs[1][0, k]
                m_in = ml_in[:, 0:1]
                m = jnp.maximum(m_in, m)
                alpha = jnp.exp2(m_in - m)
            p1 = jnp.exp2(s1 - m).astype(jnp.bfloat16)
            acc = jnp.dot(p1, vals, preferred_element_type=jnp.float32)
            l = jnp.dot(p1, ones_prompt, preferred_element_type=jnp.float32)
            if own:
                p2 = jnp.where(live, jnp.exp2(s2 - m), 0.0).astype(jnp.bfloat16)
                acc = acc + jnp.dot(p2, own_ref[1, 0, :, pl.ds(col, HEAD)], preferred_element_type=jnp.float32)
                l = l + jnp.dot(p2, ones_own, preferred_element_type=jnp.float32)
            if carry_in:
                acc = alpha * in_refs[0][0, k] + acc
                l = alpha * ml_in[:, HALF:HALF + 1] + l
            acc_ref[0, k] = acc
            lane = lax.broadcasted_iota(jnp.int32, (nrow, HEAD), 1)
            ml_ref[0, k] = jnp.where(lane < HALF, m, l)
            return carry

        lax.fori_loop(0, kv_heads, head, 0)


def resp_kernel(meta_ref, q_ref, rk_hbm, acc_ref, ml_ref, out_ref, lse_ref, kv_buf, sems,
                *, rows, groups, kv_heads, scale, block, max_blocks):
    r = pl.program_id(0)
    c = meta_ref[meta_ref.shape[0] - 1]
    length = meta_ref[r]
    live_any = length > rows * c
    nrow = rows * groups
    kv_width = groups * HEAD
    limit = jnp.minimum(rows * c, length)
    nblocks = (limit + block - 1) // block

    @pl.when(jnp.logical_not(live_any))
    def _():
        out_ref[...] = jnp.zeros(out_ref.shape, out_ref.dtype)
        lse_ref[...] = jnp.zeros(lse_ref.shape, lse_ref.dtype)

    def run(n):
        width = n * block
        if n > 0:
            chunk = rk_hbm.shape[3]
            copies = [
                pltpu.make_async_copy(rk_hbm.at[i, h, r], kv_buf.at[h, pl.ds(i * chunk, chunk), :], sems.at[h, i])
                for h in range(2)
                for i in range(width // chunk)
            ]
            for cp in copies:
                cp.start()
            for cp in copies:
                cp.wait()
        row_i = rows * c + lax.broadcasted_iota(jnp.int32, (nrow, 1), 0) % rows
        row_live = row_i < length
        ones = jnp.ones((max(width, 8), HEAD), jnp.bfloat16)

        def head(k, carry):
            col = pl.multiple_of(k * HEAD, HEAD)
            qoff = pl.multiple_of(k * kv_width, kv_width)
            ml = ml_ref[0, k]
            m = ml[:, 0:1]
            l = ml[:, HALF:HALF + 1]
            acc = acc_ref[0, k]
            if n > 0:
                qk = stack_groups(q_ref[0, :, pl.ds(qoff, kv_width)], groups)
                s = scores(qk, kv_buf[0, 0:width, pl.ds(col, HEAD)], scale)
                live = lax.broadcasted_iota(jnp.int32, (nrow, width), 1) < limit
                s = jnp.where(live, s, NEG)
                m_new = jnp.maximum(m, jnp.max(s, axis=-1, keepdims=True))
                alpha = jnp.exp2(m - m_new)
                p = jnp.where(live, jnp.exp2(s - m_new), 0.0).astype(jnp.bfloat16)
                l = alpha * l + jnp.dot(p, ones, preferred_element_type=jnp.float32)
                pv = jnp.dot(p, kv_buf[1, 0:width, pl.ds(col, HEAD)], preferred_element_type=jnp.float32)
                acc = alpha * acc + pv
                m = m_new
            o = jnp.where(row_live, acc / l, 0.0).astype(out_ref.dtype)
            for g in range(groups):
                out_ref[0, :, pl.ds(qoff + g * HEAD, HEAD)] = o[g * rows:(g + 1) * rows]
            lse = jnp.where(row_live, m * LN2 + jnp.log(l), 0.0)
            lse_ref[0, k] = jnp.broadcast_to(lse, (nrow, HEAD)).T[0:1]
            return carry

        lax.fori_loop(0, kv_heads, head, 0)

    for n in range(max_blocks + 1):
        pl.when(live_any & (nblocks == n))(functools.partial(run, n))


def per_device(queries, prompt_kv, response_kv, lengths):
    resp_local, rows, width = queries.shape
    kv_width = prompt_kv.shape[2]
    kv_heads = kv_width // HEAD
    groups = width // kv_width
    nrow = rows * groups
    scale = math.log2(math.e) / math.sqrt(HEAD)
    c = lax.axis_index("ctx")
    meta = jnp.concatenate([lengths.astype(jnp.int32), c.astype(jnp.int32)[None]])

    ctx_prompt = lax.all_gather(prompt_kv, "ctx", axis=1, tiled=True)
    n_resp_dev = lax.axis_size("resp")
    pieces = [ctx_prompt] + [
        lax.ppermute(ctx_prompt, "resp", [(j, (j + shift) % n_resp_dev) for j in range(n_resp_dev)])
        for shift in range(1, n_resp_dev)
    ]
    full_resp = lax.all_gather(response_kv, "ctx", axis=0, tiled=False)
    n_piece = ctx_prompt.shape[1]
    n_prompt = n_piece * len(pieces)
    n_resp = full_resp.shape[0] * full_resp.shape[3]

    q_spec = pl.BlockSpec((1, rows, width), lambda r, meta: (r, 0, 0))
    acc_spec = pl.BlockSpec((1, kv_heads, nrow, HEAD), lambda r, meta: (r, 0, 0, 0))

    params = pltpu.CompilerParams(vmem_limit_bytes=48 * 1024 * 1024)
    state_shape = [jax.ShapeDtypeStruct((resp_local, kv_heads, nrow, HEAD), jnp.float32)] * 2

    def prompt_pass(chunks, own, carry_in, state):
        keys_here = n_piece * len(chunks) + (rows if own else 0)
        return pl.pallas_call(
            functools.partial(prompt_kernel, rows=rows, groups=groups, kv_heads=kv_heads, scale=scale,
                              pieces=len(chunks), own=own, carry_in=carry_in),
            grid_spec=pltpu.PrefetchScalarGridSpec(
                num_scalar_prefetch=1,
                grid=(resp_local,),
                in_specs=[
                    q_spec,
                    *[pl.BlockSpec((2, n_piece, kv_width), lambda r, meta: (0, 0, 0)) for _ in chunks],
                    *([pl.BlockSpec((2, 1, rows, kv_width), lambda r, meta: (0, r, 0, 0))] if own else []),
                    *([acc_spec] * 2 if carry_in else []),
                ],
                out_specs=[acc_spec, acc_spec],
            ),
            out_shape=state_shape,
            compiler_params=params,
            cost_estimate=pl.CostEstimate(
                flops=6 * resp_local * kv_heads * nrow * keys_here * HEAD,
                transcendentals=resp_local * kv_heads * nrow * keys_here,
                bytes_accessed=2 * (queries.size + keys_here * 2 * kv_width) + 12 * resp_local * kv_heads * nrow * HEAD,
            ),
        )(meta, queries, *chunks, *([response_kv] if own else []), *state)

    first = prompt_pass(pieces[:1], True, False, [])
    acc, ml = prompt_pass(pieces[1:], False, True, list(first))

    block = 128
    max_blocks = (n_resp - rows + block - 1) // block
    attended, lse_t = pl.pallas_call(
        functools.partial(resp_kernel, rows=rows, groups=groups, kv_heads=kv_heads, scale=scale, block=block,
                          max_blocks=max_blocks),
        grid_spec=pltpu.PrefetchScalarGridSpec(
            num_scalar_prefetch=1,
            grid=(resp_local,),
            in_specs=[
                q_spec,
                pl.BlockSpec(memory_space=pl.ANY),
                acc_spec,
                acc_spec,
            ],
            out_specs=[
                q_spec,
                pl.BlockSpec((1, kv_heads, 1, nrow), lambda r, meta: (r, 0, 0, 0)),
            ],
            scratch_shapes=[
                pltpu.VMEM((2, max_blocks * block, kv_width), jnp.bfloat16),
                pltpu.SemaphoreType.DMA((2, full_resp.shape[0])),
            ],
        ),
        out_shape=[
            jax.ShapeDtypeStruct(queries.shape, queries.dtype),
            jax.ShapeDtypeStruct((resp_local, kv_heads, 1, nrow), jnp.float32),
        ],
        compiler_params=params,
        cost_estimate=pl.CostEstimate(
            flops=4 * resp_local * kv_heads * nrow * n_resp * HEAD // 2,
            transcendentals=resp_local * kv_heads * nrow * n_resp // 2,
            bytes_accessed=2 * (2 * queries.size + full_resp.size) + 4 * resp_local * kv_heads * nrow * HEAD,
        ),
    )(meta, queries, full_resp, acc, ml)

    row_lse = (
        lse_t.reshape(resp_local, kv_heads, groups, rows)
        .transpose(0, 3, 1, 2)
        .reshape(resp_local, rows, kv_heads * groups)
    )
    return attended, row_lse


def solution(mesh):
    placed = (
        P("resp", "ctx", None),
        P(None, ("resp", "ctx"), None),
        P(None, "resp", "ctx", None),
        P("resp"),
    )
    return jax.shard_map(
        per_device,
        mesh=mesh,
        in_specs=placed,
        out_specs=(P("resp", "ctx", None), P("resp", "ctx", None)),
        check_vma=False,
    )
```

```python
import functools
import math

import jax
import jax.numpy as jnp
from jax import lax
from jax.experimental import pallas as pl
from jax.experimental.pallas import tpu as pltpu
from jax.sharding import PartitionSpec as P

HEAD = 128
NEG = -1e30
LN2 = math.log(2.0)


def stack_groups(q, groups):
    return jnp.concatenate([q[:, g * HEAD:(g + 1) * HEAD] for g in range(groups)], axis=0)


def scores(qk, keys, scale):
    return lax.dot_general(qk, keys, (((1,), (1,)), ((), ())), preferred_element_type=jnp.float32) * scale


def prompt_kernel(meta_ref, q_ref, *refs, rows, groups, kv_heads, scale, pieces, own, carry_in):
    piece_refs = refs[:pieces]
    rest = list(refs[pieces:])
    own_ref = rest.pop(0) if own else None
    in_refs = [rest.pop(0) for _ in range(3)] if carry_in else None
    acc_ref, m_ref, l_ref = rest
    r = pl.program_id(0)
    c = meta_ref[meta_ref.shape[0] - 1]
    length = meta_ref[r]
    nrow = rows * groups
    kv_width = groups * HEAD

    @pl.when(length > rows * c)
    def _():
        row_i = rows * c + lax.broadcasted_iota(jnp.int32, (nrow, 1), 0) % rows
        j = rows * c + lax.broadcasted_iota(jnp.int32, (nrow, rows), 1)
        live = (j <= row_i) & (j < length)
        n_prompt = sum(p_ref.shape[1] for p_ref in piece_refs)
        ones_prompt = jnp.ones((n_prompt, HEAD), jnp.bfloat16)
        ones_own = jnp.ones((rows, HEAD), jnp.bfloat16)

        def head(k, carry):
            col = pl.multiple_of(k * HEAD, HEAD)
            qk = stack_groups(q_ref[0, :, pl.ds(pl.multiple_of(k * kv_width, kv_width), kv_width)], groups)
            keys = jnp.concatenate([p_ref[0, :, pl.ds(col, HEAD)] for p_ref in piece_refs], axis=0)
            vals = jnp.concatenate([p_ref[1, :, pl.ds(col, HEAD)] for p_ref in piece_refs], axis=0)
            s1 = scores(qk, keys, scale)
            m = jnp.max(s1, axis=-1, keepdims=True)
            if own:
                s2 = jnp.where(live, scores(qk, own_ref[0, 0, :, pl.ds(col, HEAD)], scale), NEG)
                m = jnp.maximum(m, jnp.max(s2, axis=-1, keepdims=True))
            if carry_in:
                m_in = in_refs[1][0, k]
                m = jnp.maximum(m_in[:, 0:1], m)
                alpha = jnp.exp2(m_in - m)
            m_rep = jnp.broadcast_to(m, (nrow, HEAD))
            p1 = jnp.exp2(s1 - m).astype(jnp.bfloat16)
            acc = jnp.dot(p1, vals, preferred_element_type=jnp.float32)
            l = jnp.dot(p1, ones_prompt, preferred_element_type=jnp.float32)
            if own:
                p2 = jnp.where(live, jnp.exp2(s2 - m), 0.0).astype(jnp.bfloat16)
                acc = acc + jnp.dot(p2, own_ref[1, 0, :, pl.ds(col, HEAD)], preferred_element_type=jnp.float32)
                l = l + jnp.dot(p2, ones_own, preferred_element_type=jnp.float32)
            if carry_in:
                acc = alpha * in_refs[0][0, k] + acc
                l = alpha * in_refs[2][0, k] + l
            acc_ref[0, k] = acc
            m_ref[0, k] = m_rep
            l_ref[0, k] = l
            return carry

        lax.fori_loop(0, kv_heads, head, 0)


def resp_kernel(meta_ref, q_ref, rk_hbm, acc_ref, m_ref, l_ref, out_ref, lse_ref, kv_buf, sems,
                *, rows, groups, kv_heads, scale, block, max_blocks):
    r = pl.program_id(0)
    c = meta_ref[meta_ref.shape[0] - 1]
    length = meta_ref[r]
    live_any = length > rows * c
    nrow = rows * groups
    kv_width = groups * HEAD
    limit = jnp.minimum(rows * c, length)
    nblocks = (limit + block - 1) // block

    @pl.when(jnp.logical_not(live_any))
    def _():
        out_ref[...] = jnp.zeros(out_ref.shape, out_ref.dtype)
        lse_ref[...] = jnp.zeros(lse_ref.shape, lse_ref.dtype)

    def run(n):
        width = n * block
        if n > 0:
            chunk = rk_hbm.shape[3]
            copies = [
                pltpu.make_async_copy(rk_hbm.at[i, h, r], kv_buf.at[h, pl.ds(i * chunk, chunk), :], sems.at[h, i])
                for h in range(2)
                for i in range(width // chunk)
            ]
            for cp in copies:
                cp.start()
            for cp in copies:
                cp.wait()
        row_i = rows * c + lax.broadcasted_iota(jnp.int32, (nrow, 1), 0) % rows
        row_live = row_i < length
        ones = jnp.ones((max(width, 8), HEAD), jnp.bfloat16)

        def head(k, carry):
            col = pl.multiple_of(k * HEAD, HEAD)
            qoff = pl.multiple_of(k * kv_width, kv_width)
            m = m_ref[0, k]
            l = l_ref[0, k]
            acc = acc_ref[0, k]
            if n > 0:
                qk = stack_groups(q_ref[0, :, pl.ds(qoff, kv_width)], groups)
                s = scores(qk, kv_buf[0, 0:width, pl.ds(col, HEAD)], scale)
                live = lax.broadcasted_iota(jnp.int32, (nrow, width), 1) < limit
                s = jnp.where(live, s, NEG)
                m_new = jnp.maximum(m, jnp.max(s, axis=-1, keepdims=True))
                alpha = jnp.exp2(m - m_new)
                m_wide = m_new if n == 1 else jnp.concatenate([m_new] * n, axis=1)
                p = jnp.where(live, jnp.exp2(s - m_wide), 0.0).astype(jnp.bfloat16)
                l = alpha * l + jnp.dot(p, ones, preferred_element_type=jnp.float32)
                pv = jnp.dot(p, kv_buf[1, 0:width, pl.ds(col, HEAD)], preferred_element_type=jnp.float32)
                acc = alpha * acc + pv
                m = m_new
            o = jnp.where(row_live, acc / l, 0.0).astype(out_ref.dtype)
            for g in range(groups):
                out_ref[0, :, pl.ds(qoff + g * HEAD, HEAD)] = o[g * rows:(g + 1) * rows]
            lse = jnp.where(row_live, m * LN2 + jnp.log(l), 0.0)
            lse_ref[0, k] = lse.T[0:1]
            return carry

        lax.fori_loop(0, kv_heads, head, 0)

    for n in range(max_blocks + 1):
        pl.when(live_any & (nblocks == n))(functools.partial(run, n))


def per_device(queries, prompt_kv, response_kv, lengths):
    resp_local, rows, width = queries.shape
    kv_width = prompt_kv.shape[2]
    kv_heads = kv_width // HEAD
    groups = width // kv_width
    nrow = rows * groups
    scale = math.log2(math.e) / math.sqrt(HEAD)
    c = lax.axis_index("ctx")
    meta = jnp.concatenate([lengths.astype(jnp.int32), c.astype(jnp.int32)[None]])

    ctx_prompt = lax.all_gather(prompt_kv, "ctx", axis=1, tiled=True)
    n_resp_dev = lax.axis_size("resp")
    pieces = [ctx_prompt] + [
        lax.ppermute(ctx_prompt, "resp", [(j, (j + shift) % n_resp_dev) for j in range(n_resp_dev)])
        for shift in range(1, n_resp_dev)
    ]
    full_resp = lax.all_gather(response_kv, "ctx", axis=0, tiled=False)
    n_piece = ctx_prompt.shape[1]
    n_prompt = n_piece * len(pieces)
    n_resp = full_resp.shape[0] * full_resp.shape[3]

    q_spec = pl.BlockSpec((1, rows, width), lambda r, meta: (r, 0, 0))
    acc_spec = pl.BlockSpec((1, kv_heads, nrow, HEAD), lambda r, meta: (r, 0, 0, 0))

    params = pltpu.CompilerParams(vmem_limit_bytes=48 * 1024 * 1024)
    state_shape = [jax.ShapeDtypeStruct((resp_local, kv_heads, nrow, HEAD), jnp.float32)] * 3

    def prompt_pass(chunks, own, carry_in, state):
        keys_here = n_piece * len(chunks) + (rows if own else 0)
        return pl.pallas_call(
            functools.partial(prompt_kernel, rows=rows, groups=groups, kv_heads=kv_heads, scale=scale,
                              pieces=len(chunks), own=own, carry_in=carry_in),
            grid_spec=pltpu.PrefetchScalarGridSpec(
                num_scalar_prefetch=1,
                grid=(resp_local,),
                in_specs=[
                    q_spec,
                    *[pl.BlockSpec((2, n_piece, kv_width), lambda r, meta: (0, 0, 0)) for _ in chunks],
                    *([pl.BlockSpec((2, 1, rows, kv_width), lambda r, meta: (0, r, 0, 0))] if own else []),
                    *([acc_spec] * 3 if carry_in else []),
                ],
                out_specs=[acc_spec, acc_spec, acc_spec],
            ),
            out_shape=state_shape,
            compiler_params=params,
            cost_estimate=pl.CostEstimate(
                flops=6 * resp_local * kv_heads * nrow * keys_here * HEAD,
                transcendentals=resp_local * kv_heads * nrow * keys_here,
                bytes_accessed=2 * (queries.size + keys_here * 2 * kv_width) + 12 * resp_local * kv_heads * nrow * HEAD,
            ),
        )(meta, queries, *chunks, *([response_kv] if own else []), *state)

    first = prompt_pass(pieces[:4], True, False, [])
    acc, m_rep, l_rep = prompt_pass(pieces[4:], False, True, list(first))

    block = 128
    max_blocks = (n_resp - rows + block - 1) // block
    attended, lse_t = pl.pallas_call(
        functools.partial(resp_kernel, rows=rows, groups=groups, kv_heads=kv_heads, scale=scale, block=block,
                          max_blocks=max_blocks),
        grid_spec=pltpu.PrefetchScalarGridSpec(
            num_scalar_prefetch=1,
            grid=(resp_local,),
            in_specs=[
                q_spec,
                pl.BlockSpec(memory_space=pl.ANY),
                acc_spec,
                acc_spec,
                acc_spec,
            ],
            out_specs=[
                q_spec,
                pl.BlockSpec((1, kv_heads, 1, nrow), lambda r, meta: (r, 0, 0, 0)),
            ],
            scratch_shapes=[
                pltpu.VMEM((2, max_blocks * block, kv_width), jnp.bfloat16),
                pltpu.SemaphoreType.DMA((2, full_resp.shape[0])),
            ],
        ),
        out_shape=[
            jax.ShapeDtypeStruct(queries.shape, queries.dtype),
            jax.ShapeDtypeStruct((resp_local, kv_heads, 1, nrow), jnp.float32),
        ],
        compiler_params=params,
        cost_estimate=pl.CostEstimate(
            flops=4 * resp_local * kv_heads * nrow * n_resp * HEAD // 2,
            transcendentals=resp_local * kv_heads * nrow * n_resp // 2,
            bytes_accessed=2 * (2 * queries.size + full_resp.size) + 4 * resp_local * kv_heads * nrow * HEAD,
        ),
    )(meta, queries, full_resp, acc, m_rep, l_rep)

    row_lse = (
        lse_t.reshape(resp_local, kv_heads, groups, rows)
        .transpose(0, 3, 1, 2)
        .reshape(resp_local, rows, kv_heads * groups)
    )
    return attended, row_lse


def solution(mesh):
    placed = (
        P("resp", "ctx", None),
        P(None, ("resp", "ctx"), None),
        P(None, "resp", "ctx", None),
        P("resp"),
    )
    return jax.shard_map(
        per_device,
        mesh=mesh,
        in_specs=placed,
        out_specs=(P("resp", "ctx", None), P("resp", "ctx", None)),
        check_vma=False,
    )
```
